256 devices in a mesh: dom: 64 (over y, z, core), group: 4 (over x).
Axes of the slice: x: 4, y: 4, z: 8, core: 2. Of those that a mesh axis runs over, the one named last changes fastest.
Arguments:
- embeddings: float32 [65536, 400], P(('dom', 'group')), may hold values from -3 to 3
- adagrad_state: float32 [65536], P(('dom', 'group')), may hold values from 0.05 to 0.5
- relation_diag: float32 [64, 400], replicated, may hold values from 0.1 to 1.9
- bucket_counts: int32 [2, 64], P(None, 'dom'), may hold values from 512 to 4096, as said below
- src_index: int32 [2, 64, 4096], P(None, 'dom', 'group'), may hold values from 0 to 1023
- dst_index: int32 [2, 64, 4096], P(None, 'dom', 'group'), may hold values from 0 to 1023
- rel_index: int32 [2, 64, 4096], P(None, 'dom', 'group'), may hold values from 0 to 63
- neg_index: int32 [2, 64, 4, 1024], P(None, 'dom', 'group'), may hold values from 0 to 1023
Outputs:
- new_embeddings: float32 [65536, 400], P(('dom', 'group'))
- new_state: float32 [65536], P(('dom', 'group'))
The draws below stay inside these ranges and needn't reach their ends.
Inputs may be any that keep to these rules, and one draw needn't show every extreme that they name: bucket_counts holds the live edges of each bucket; live slots are the first ones of the bucket; at least one bucket is full and at least one holds exactly 512 live edges.
All inputs are finite; a program needn't handle non-finite values.
Results may differ from the reference program's by a relative error of at most 0.0016.
Values may be sent and summed in bfloat16 or wider, within the bound.
No kernel may reach another device: no remote copies, remote signals or barrier semaphores. Data moves between devices by JAX's collectives and lax.ppermute only.
A program may use at most 64 MiB of HBM per device.

```python
import math
from functools import partial
import jax
import jax.numpy as jnp
from jax import lax

D = 400
EDGE_DEV = 1024
NEG = 1024
ROUNDS = 2
RELS = 64
PART = 1024
EDGES = 4096
ENT = 65536
N_DOM = 64
N_GROUP = 4


def draw_bucket_counts(key, part):
    key_base, key_pick = jax.random.split(key, 2)
    counts = jax.random.randint(key_base, (ROUNDS, N_DOM), EDGES // 8, EDGES + 1)
    flat_counts = counts.reshape(-1)
    picked = jax.random.permutation(key_pick, ROUNDS * N_DOM)
    flat_counts = flat_counts.at[picked[0]].set(EDGES).at[picked[1]].set(EDGES // 8)
    return flat_counts.reshape(ROUNDS, N_DOM).astype(jnp.int32)


def with_ends(result, stream_key, low, top_value):
    longest = result.shape.index(max(result.shape))
    spots = []
    for shift in (0, 1):
        where = [jax.random.randint(jax.random.fold_in(stream_key, axis), (), 0, length) for axis, length in enumerate(result.shape)]
        where[longest] = (where[longest] + shift) % result.shape[longest]
        spots.append(tuple(where))
    return result.at[spots[0]].set(low).at[spots[1]].set(top_value)


def shard_levels(key, dims, pieces, smallest, high):
    def one(position, blocks):
        steps = jax.random.uniform(jax.random.fold_in(jax.random.fold_in(key, 6), position), (blocks,), jnp.float32, smallest / len(pieces), high / len(pieces))
        return jnp.repeat(jnp.exp(steps), dims[position] // blocks).reshape((-1,) + (1,) * (len(dims) - position - 1))

    factor_of = one(*pieces[0])
    for cut in pieces[1:]:
        factor_of = factor_of * one(*cut)
    return factor_of


def centred(stream_key, shape, spread, limit, cuts=(), kind=jnp.bfloat16):
    drawn = jax.random.normal(stream_key, shape, jnp.float32) * spread
    if len(cuts) > 0:
        drawn = shard_levels(stream_key, shape, cuts, -0.22, 0.18) * drawn
    return jnp.clip(drawn, min=-limit, max=limit).astype(kind)


def setup_inputs(seed: int = 0) -> dict:
    streams_of = jax.random.split(jax.random.key(seed), 9)
    return {
        "embeddings": centred(streams_of[0], (ENT, D), 0.5, 3.0, ((0, 256),), jnp.float32),
        "adagrad_state": jnp.clip(jnp.exp(math.log(0.5) - 2.3025851 * jax.random.uniform(streams_of[1], (ENT,), jnp.float32) ** shard_levels(streams_of[1], (ENT,), ((0, 256),), -0.2, 0.2)), 0.05, 0.5),
        "relation_diag": jnp.clip(1.0 + 0.18 * jax.random.normal(streams_of[2], (RELS, D), jnp.float32), 0.1, 1.9),
        "bucket_counts": draw_bucket_counts(jax.random.fold_in(streams_of[8], 71), 0),
        "src_index": with_ends(jax.random.randint(streams_of[4], (ROUNDS, N_DOM, EDGES), 0, PART), jax.random.fold_in(streams_of[4], 1), 0, PART - 1).astype(jnp.int32),
        "dst_index": with_ends(jax.random.randint(streams_of[5], (ROUNDS, N_DOM, EDGES), 0, PART), jax.random.fold_in(streams_of[5], 1), 0, PART - 1).astype(jnp.int32),
        "rel_index": with_ends(jax.random.randint(streams_of[6], (ROUNDS, N_DOM, EDGES), 0, RELS), jax.random.fold_in(streams_of[6], 1), 0, RELS - 1).astype(jnp.int32),
        "neg_index": with_ends(jax.random.randint(streams_of[7], (ROUNDS, N_DOM, N_GROUP, NEG), 0, PART), jax.random.fold_in(streams_of[7], 1), 0, PART - 1).astype(jnp.int32),
    }


LEARN_RATE = 0.1
ROW_EPS = 1e-06

def block_terms(lhs_block, rhs_block, relation_diag, src_ids, dst_ids, rel_ids, neg_ids, live_mask):
    lhs_rows = jnp.take(lhs_block, src_ids, axis=0).astype(jnp.float32)
    rhs_rows = jnp.take(rhs_block, dst_ids, axis=0).astype(jnp.float32)
    neg_rows = jnp.take(rhs_block, neg_ids, axis=0).astype(jnp.float32)
    rel_rows = jnp.take(relation_diag, rel_ids, axis=0)
    query_rows = lhs_rows * rel_rows
    query_half = lax.optimization_barrier(query_rows.astype(jnp.bfloat16)).astype(jnp.float32)
    pos_score = lax.optimization_barrier(jnp.sum(query_rows * rhs_rows, axis=1))
    scores = jnp.dot(query_half, neg_rows.T, precision=lax.Precision.HIGHEST)
    weights = (live_mask[:, None] * jax.nn.sigmoid(scores) / NEG).astype(jnp.bfloat16)
    weights = lax.optimization_barrier(weights).astype(jnp.float32)
    pos_coef = -live_mask * jax.nn.sigmoid(-pos_score)
    grad_query = pos_coef[:, None] * rhs_rows + jnp.dot(weights, neg_rows, precision=lax.Precision.HIGHEST)
    grad_neg = jnp.dot(weights.T, query_half, precision=lax.Precision.HIGHEST)
    return (grad_query * rel_rows, pos_coef[:, None] * query_rows, grad_neg)

def reference(embeddings, adagrad_state, relation_diag, bucket_counts, src_index, dst_index, rel_index, neg_index):
    emb_half = embeddings.astype(jnp.bfloat16)
    blocks = emb_half.reshape(N_DOM, PART, D)
    slot_ids = jnp.arange(EDGES, dtype=jnp.int32).reshape(N_GROUP, EDGE_DEV)

    def worker(loop_index, grad_table):
        worker_id = jnp.asarray(loop_index).astype(jnp.int32)
        lhs_block = lax.dynamic_index_in_dim(blocks, worker_id, 0, keepdims=False)
        for turn_index in range(ROUNDS):
            far_part = jnp.mod(worker_id - (turn_index + 1), N_DOM).astype(jnp.int32)
            rhs_block = lax.dynamic_index_in_dim(blocks, far_part, 0, keepdims=False)
            live_count = lax.dynamic_index_in_dim(bucket_counts[turn_index], worker_id, 0, keepdims=False)
            live_mask = (slot_ids < live_count).astype(jnp.float32)
            src_ids = lax.dynamic_index_in_dim(src_index[turn_index], worker_id, 0, keepdims=False).reshape(N_GROUP, EDGE_DEV)
            dst_ids = lax.dynamic_index_in_dim(dst_index[turn_index], worker_id, 0, keepdims=False).reshape(N_GROUP, EDGE_DEV)
            rel_ids = lax.dynamic_index_in_dim(rel_index[turn_index], worker_id, 0, keepdims=False).reshape(N_GROUP, EDGE_DEV)
            neg_ids = lax.dynamic_index_in_dim(neg_index[turn_index], worker_id, 0, keepdims=False)
            terms = jax.vmap(partial(block_terms, lhs_block, rhs_block, relation_diag))(src_ids, dst_ids, rel_ids, neg_ids, live_mask)
            lhs_sum = jax.ops.segment_sum(terms[0].reshape(-1, D), src_ids.reshape(-1), PART)
            rhs_sum = jax.ops.segment_sum(terms[1].reshape(-1, D), dst_ids.reshape(-1), PART)
            rhs_sum = rhs_sum + jax.ops.segment_sum(terms[2].reshape(-1, D), neg_ids.reshape(-1), PART)
            grad_table = grad_table.at[worker_id].add(lhs_sum)
            grad_table = grad_table.at[far_part].add(rhs_sum)
        return grad_table
    grad_table = lax.fori_loop(0, N_DOM, worker, jnp.zeros((N_DOM, PART, D), jnp.float32))
    grad_total = grad_table.reshape(ENT, D)
    new_state = adagrad_state + lax.optimization_barrier(jnp.mean(grad_total * grad_total, axis=1))
    new_embeddings = embeddings - LEARN_RATE * grad_total / (jnp.sqrt(new_state)[:, None] + ROW_EPS)
    return (new_embeddings, new_state)
```

```python
import jax
import jax.numpy as jnp
from jax import lax
from jax.sharding import PartitionSpec as P

ROUNDS = 2
GATHER_AXIS = 1


LEARN_RATE = 0.1
ROW_EPS = 1e-06


def from_behind(block, axis, distance):
    devices = range(lax.axis_size(axis))
    route = [((i - distance) % len(devices), i) for i in devices]
    return lax.ppermute(block, axis, route)


def select_table(row_ids, count):
    return row_ids[:, None] == lax.iota(jnp.int32, count)[None, :]


def pick_rows(table, block):
    return jnp.dot(table.astype(jnp.bfloat16), block, preferred_element_type=jnp.float32).astype(
        jnp.bfloat16
    )


def add_rows(table, values):
    return lax.dot_general(
        table.astype(jnp.float32), values, (((0,), (0,)), ((), ())), precision=lax.Precision.HIGHEST
    )


def block_grads(lhs_block, rhs_block, relation_diag, src_ids, dst_ids, rel_ids, neg_ids, live_mask):
    part_rows = lhs_block.shape[0]
    src_table = select_table(src_ids, part_rows)
    dst_table = select_table(dst_ids, part_rows)
    neg_table = select_table(neg_ids, part_rows)
    lhs_rows = pick_rows(src_table, lhs_block)
    rhs_rows = pick_rows(dst_table, rhs_block)
    neg_rows = pick_rows(neg_table, rhs_block)
    relation_count = relation_diag.shape[0]
    onehot = select_table(rel_ids, relation_count).astype(jnp.float32)
    rel_rows = jnp.dot(onehot, relation_diag, precision=lax.Precision.HIGHEST)
    query_rows = lhs_rows.astype(jnp.float32) * rel_rows
    query_half = query_rows.astype(jnp.bfloat16)
    rhs_wide = rhs_rows.astype(jnp.float32)
    pos_score = jnp.sum(query_rows * rhs_wide, axis=1)
    scores = lax.dot_general(
        query_half, neg_rows, (((1,), (1,)), ((), ())), preferred_element_type=jnp.float32
    )
    weights = (live_mask[:, None] * jax.nn.sigmoid(scores) / neg_ids.shape[0]).astype(jnp.bfloat16)
    pos_coef = -live_mask * jax.nn.sigmoid(-pos_score)
    grad_query = pos_coef[:, None] * rhs_wide + jnp.dot(
        weights, neg_rows, preferred_element_type=jnp.float32
    )
    grad_neg = lax.dot_general(
        weights, query_half, (((0,), (0,)), ((), ())), preferred_element_type=jnp.float32
    )
    lhs_grad = add_rows(src_table, grad_query * rel_rows)
    both_tables = jnp.concatenate([dst_table, neg_table], axis=0)
    both_terms = jnp.concatenate([pos_coef[:, None] * query_rows, grad_neg], axis=0)
    rhs_grad = add_rows(both_tables, both_terms)
    return (lhs_grad, rhs_grad)


def per_device(
    embeddings,
    adagrad_state,
    relation_diag,
    bucket_counts,
    src_index,
    dst_index,
    rel_index,
    neg_index,
):
    emb_half = embeddings.astype(jnp.bfloat16)
    quarter = emb_half.shape[0]
    emb_width = embeddings.shape[1]
    parts = [emb_half] + [from_behind(emb_half, "dom", k + 1) for k in range(ROUNDS)]
    stacked = jnp.stack(parts)
    gathered = lax.all_gather(stacked, "group", axis=GATHER_AXIS, tiled=False)
    n_group = lax.axis_size("group")
    if GATHER_AXIS == 0:
        blocks = jnp.transpose(gathered, (1, 0, 2, 3)).reshape(ROUNDS + 1, n_group * quarter, emb_width)
    else:
        blocks = gathered.reshape(ROUNDS + 1, n_group * quarter, emb_width)
    own_block = blocks[0]
    part_rows = own_block.shape[0]
    edge_slots = src_index.shape[2]
    slot_ids = lax.axis_index("group") * edge_slots + lax.iota(jnp.int32, edge_slots)
    lhs_partial = jnp.zeros((part_rows, emb_width), jnp.float32)
    for turn_index in range(ROUNDS):
        shift_by = turn_index + 1
        rhs_block = blocks[shift_by]
        live_mask = (slot_ids < bucket_counts[turn_index, 0]).astype(jnp.float32)
        lhs_grad, rhs_grad = block_grads(
            own_block,
            rhs_block,
            relation_diag,
            src_index[turn_index, 0],
            dst_index[turn_index, 0],
            rel_index[turn_index, 0],
            neg_index[turn_index, 0, 0],
            live_mask,
        )
        lhs_partial = lhs_partial + lhs_grad
        lhs_partial = lhs_partial + from_behind(rhs_grad, "dom", -shift_by)
    grad_total = lax.psum_scatter(lhs_partial, "group", scatter_dimension=0, tiled=True)
    new_state = adagrad_state + jnp.mean(grad_total * grad_total, axis=1)
    new_embeddings = embeddings - LEARN_RATE * grad_total / (jnp.sqrt(new_state)[:, None] + ROW_EPS)
    return (new_embeddings, new_state)


def solution(mesh):
    placed = (
        P(("dom", "group"), None),
        P(("dom", "group")),
        P(),
        P(None, "dom"),
        P(None, "dom", "group"),
        P(None, "dom", "group"),
        P(None, "dom", "group"),
        P(None, "dom", "group", None),
    )
    return jax.shard_map(
        per_device,
        mesh=mesh,
        in_specs=placed,
        out_specs=(P(("dom", "group"), None), P(("dom", "group"))),
        check_vma=False,
    )
```

```python
import jax
import jax.numpy as jnp
from jax import lax
from jax.sharding import PartitionSpec as P

ROUNDS = 2


LEARN_RATE = 0.1
ROW_EPS = 1e-06


def from_behind(block, axis, distance):
    devices = range(lax.axis_size(axis))
    route = [((i - distance) % len(devices), i) for i in devices]
    return lax.ppermute(block, axis, route)


def parity_swap(block, axis, distance):
    n = lax.axis_size(axis)
    route = [((i - distance) % n, i) if i % 2 == 0 else ((i + distance) % n, i) for i in range(n)]
    return lax.ppermute(block, axis, route)


def parity_return(block, axis, distance):
    n = lax.axis_size(axis)
    route = [(i, (i - distance) % n) if i % 2 == 0 else (i, (i + distance) % n) for i in range(n)]
    return lax.ppermute(block, axis, route)


def group_gather(x):
    half = x.shape[1] // 2
    p1 = from_behind(x, "group", 1)
    p3 = from_behind(x, "group", -1)
    p2a = from_behind(p1[:, :half], "group", 1)
    p2b = from_behind(p3[:, half:], "group", -1)
    return jnp.concatenate([x, p1, p2a, p2b, p3], axis=1)


def group_reduce_scatter(y, quarter):
    half = quarter // 2
    c0, c1, c2, c3 = (y[s * quarter:(s + 1) * quarter] for s in range(4))
    s1a = from_behind(c2[:half], "group", 1)
    s1b = from_behind(c3[half:], "group", 1)
    t1a = from_behind(c2[half:], "group", -1)
    t1b = from_behind(c1[:half], "group", -1)
    s2a = from_behind(s1a + c3[:half], "group", 1)
    t2a = from_behind(t1a + c1[half:], "group", -1)
    top = c0[:half] + s2a + t1b
    bottom = c0[half:] + s1b + t2a
    return jnp.concatenate([top, bottom], axis=0)


def select_table(row_ids, count):
    return row_ids[:, None] == lax.iota(jnp.int32, count)[None, :]


def pick_rows(table, block):
    return jnp.dot(table.astype(jnp.bfloat16), block, preferred_element_type=jnp.float32).astype(
        jnp.bfloat16
    )


def add_rows(table, values):
    hi = values.astype(jnp.bfloat16)
    lo = (values - hi.astype(jnp.float32)).astype(jnp.bfloat16)
    both = jnp.concatenate([hi, lo], axis=1)
    summed = lax.dot_general(
        table.astype(jnp.bfloat16), both, (((0,), (0,)), ((), ())), preferred_element_type=jnp.float32
    )
    width = values.shape[1]
    return summed[:, :width] + summed[:, width:]


def block_grads(lhs_block, rhs_block, relation_diag, src_ids, dst_ids, rel_ids, neg_ids, live_mask):
    part_rows = lhs_block.shape[0]
    src_table = select_table(src_ids, part_rows)
    dst_table = select_table(dst_ids, part_rows)
    neg_table = select_table(neg_ids, part_rows)
    lhs_rows = pick_rows(src_table, lhs_block)
    rhs_rows = pick_rows(dst_table, rhs_block)
    neg_rows = pick_rows(neg_table, rhs_block)
    relation_count = relation_diag.shape[0]
    onehot = select_table(rel_ids, relation_count).astype(jnp.float32)
    rel_rows = jnp.dot(onehot, relation_diag, precision=lax.Precision.HIGHEST)
    query_rows = lhs_rows.astype(jnp.float32) * rel_rows
    query_half = query_rows.astype(jnp.bfloat16)
    rhs_wide = rhs_rows.astype(jnp.float32)
    pos_score = jnp.sum(query_rows * rhs_wide, axis=1)
    scores = lax.dot_general(
        query_half, neg_rows, (((1,), (1,)), ((), ())), preferred_element_type=jnp.float32
    )
    weights = (live_mask[:, None] * jax.nn.sigmoid(scores) / neg_ids.shape[0]).astype(jnp.bfloat16)
    pos_coef = -live_mask * jax.nn.sigmoid(-pos_score)
    grad_query = pos_coef[:, None] * rhs_wide + jnp.dot(
        weights, neg_rows, preferred_element_type=jnp.float32
    )
    grad_neg = lax.dot_general(
        weights, query_half, (((0,), (0,)), ((), ())), preferred_element_type=jnp.float32
    )
    lhs_grad = add_rows(src_table, grad_query * rel_rows)
    both_tables = jnp.concatenate([dst_table, neg_table], axis=0)
    both_terms = jnp.concatenate([pos_coef[:, None] * query_rows, grad_neg], axis=0)
    rhs_grad = add_rows(both_tables, both_terms)
    return (lhs_grad, rhs_grad)


def per_device(
    embeddings,
    adagrad_state,
    relation_diag,
    bucket_counts,
    src_index,
    dst_index,
    rel_index,
    neg_index,
):
    emb_half = embeddings.astype(jnp.bfloat16)
    quarter = emb_half.shape[0]
    n_group = lax.axis_size("group")
    part_rows = n_group * quarter
    g = lax.axis_index("group")
    odd = (lax.axis_index("dom") % 2) == 1

    def local_rows(ids):
        return ((g - ids // quarter) % n_group) * quarter + ids % quarter

    edge_slots = src_index.shape[2]
    slot_ids = g * edge_slots + lax.iota(jnp.int32, edge_slots)

    far1 = from_behind(emb_half, "dom", 1)
    other2 = parity_swap(emb_half, "dom", 2)
    first = group_gather(jnp.stack([emb_half, far1]))
    own_block = first[0]
    rhs_block1 = first[1]
    other_block2 = group_gather(other2[None])[0]

    ids2 = jnp.stack(
        [src_index[1, 0], dst_index[1, 0], rel_index[1, 0], neg_index[1, 0, 0],
         jnp.broadcast_to(bucket_counts[1, 0], (edge_slots,))]
    )
    ids2_far = from_behind(ids2, "dom", -2)
    ids2 = jnp.where(odd, ids2_far, ids2)

    live1 = (slot_ids < bucket_counts[0, 0]).astype(jnp.float32)
    lhs_grad1, rhs_grad1 = block_grads(
        own_block,
        rhs_block1,
        relation_diag,
        local_rows(src_index[0, 0]),
        local_rows(dst_index[0, 0]),
        rel_index[0, 0],
        local_rows(neg_index[0, 0, 0]),
        live1,
    )
    recv1 = from_behind(rhs_grad1, "dom", -1)

    live2 = (slot_ids < ids2[4]).astype(jnp.float32)
    lhs_block2 = jnp.where(odd, other_block2, own_block)
    rhs_block2 = jnp.where(odd, own_block, other_block2)
    lhs_grad2, rhs_grad2 = block_grads(
        lhs_block2,
        rhs_block2,
        relation_diag,
        local_rows(ids2[0]),
        local_rows(ids2[1]),
        ids2[2],
        local_rows(ids2[3]),
        live2,
    )
    keep2 = jnp.where(odd, rhs_grad2, lhs_grad2)
    send2 = jnp.where(odd, lhs_grad2, rhs_grad2)
    recv2 = parity_return(send2, "dom", 2)

    stacked_total = lhs_grad1 + keep2 + recv1 + recv2
    grad_total = group_reduce_scatter(stacked_total, quarter)
    new_state = adagrad_state + jnp.mean(grad_total * grad_total, axis=1)
    new_embeddings = embeddings - LEARN_RATE * grad_total / (jnp.sqrt(new_state)[:, None] + ROW_EPS)
    return (new_embeddings, new_state)


def solution(mesh):
    placed = (
        P(("dom", "group"), None),
        P(("dom", "group")),
        P(),
        P(None, "dom"),
        P(None, "dom", "group"),
        P(None, "dom", "group"),
        P(None, "dom", "group"),
        P(None, "dom", "group", None),
    )
    return jax.shard_map(
        per_device,
        mesh=mesh,
        in_specs=placed,
        out_specs=(P(("dom", "group"), None), P(("dom", "group"))),
        check_vma=False,
    )
```

```python
import jax
import jax.numpy as jnp
from jax import lax
from jax.sharding import PartitionSpec as P

ROUNDS = 2


LEARN_RATE = 0.1
ROW_EPS = 1e-06


def from_behind(block, axis, distance):
    devices = range(lax.axis_size(axis))
    route = [((i - distance) % len(devices), i) for i in devices]
    return lax.ppermute(block, axis, route)


def parity_swap(block, axis, distance):
    n = lax.axis_size(axis)
    route = [((i - distance) % n, i) if i % 2 == 0 else ((i + distance) % n, i) for i in range(n)]
    return lax.ppermute(block, axis, route)


def parity_return(block, axis, distance):
    n = lax.axis_size(axis)
    route = [(i, (i - distance) % n) if i % 2 == 0 else (i, (i + distance) % n) for i in range(n)]
    return lax.ppermute(block, axis, route)


def group_gather(x):
    half = x.shape[1] // 2
    p1 = from_behind(x, "group", 1)
    p3 = from_behind(x, "group", -1)
    p2a = from_behind(p1[:, :half], "group", 1)
    p2b = from_behind(p3[:, half:], "group", -1)
    return jnp.concatenate([x, p1, p2a, p2b, p3], axis=1)


def group_reduce_scatter(y, quarter):
    half = quarter // 2
    c0, c1, c2, c3 = (y[s * quarter:(s + 1) * quarter] for s in range(4))
    plus1 = from_behind(jnp.concatenate([c2[:half], c3[half:]]), "group", 1)
    minus1 = from_behind(jnp.concatenate([c2[half:], c1[:half]]), "group", -1)
    plus2 = from_behind(plus1[:half] + c3[:half], "group", 1)
    minus2 = from_behind(minus1[:half] + c1[half:], "group", -1)
    top = c0[:half] + plus2 + minus1[half:]
    bottom = c0[half:] + plus1[half:] + minus2
    return jnp.concatenate([top, bottom], axis=0)


def select_table(row_ids, count):
    return row_ids[:, None] == lax.iota(jnp.int32, count)[None, :]


def pick_rows(table, block):
    return jnp.dot(table.astype(jnp.bfloat16), block, preferred_element_type=jnp.float32).astype(
        jnp.bfloat16
    )


def add_rows(table, values):
    hi_wide = lax.reduce_precision(values, exponent_bits=8, mantissa_bits=7)
    hi = hi_wide.astype(jnp.bfloat16)
    lo = (values - hi_wide).astype(jnp.bfloat16)
    both = jnp.concatenate([hi, lo], axis=1)
    summed = lax.dot_general(
        table.astype(jnp.bfloat16), both, (((0,), (0,)), ((), ())), preferred_element_type=jnp.float32
    )
    width = values.shape[1]
    return summed[:, :width] + summed[:, width:]


def block_grads(lhs_block, rhs_block, relation_diag, src_ids, dst_ids, rel_ids, neg_ids, live_mask):
    part_rows = lhs_block.shape[0]
    src_table = select_table(src_ids, part_rows)
    dst_table = select_table(dst_ids, part_rows)
    neg_table = select_table(neg_ids, part_rows)
    lhs_rows = pick_rows(src_table, lhs_block)
    rhs_rows = pick_rows(dst_table, rhs_block)
    neg_rows = pick_rows(neg_table, rhs_block)
    relation_count = relation_diag.shape[0]
    onehot = select_table(rel_ids, relation_count).astype(jnp.float32)
    rel_rows = jnp.dot(onehot, relation_diag, precision=lax.Precision.HIGHEST)
    query_rows = lhs_rows.astype(jnp.float32) * rel_rows
    query_half = query_rows.astype(jnp.bfloat16)
    rhs_wide = rhs_rows.astype(jnp.float32)
    pos_score = jnp.sum(query_rows * rhs_wide, axis=1)
    scores = lax.dot_general(
        query_half, neg_rows, (((1,), (1,)), ((), ())), preferred_element_type=jnp.float32
    )
    weights = (live_mask[:, None] * jax.nn.sigmoid(scores) / neg_ids.shape[0]).astype(jnp.bfloat16)
    pos_coef = -live_mask * jax.nn.sigmoid(-pos_score)
    grad_query = pos_coef[:, None] * rhs_wide + jnp.dot(
        weights, neg_rows, preferred_element_type=jnp.float32
    )
    grad_neg = lax.dot_general(
        weights, query_half, (((0,), (0,)), ((), ())), preferred_element_type=jnp.float32
    )
    lhs_grad = add_rows(src_table, grad_query * rel_rows)
    both_tables = jnp.concatenate([dst_table, neg_table], axis=0)
    both_terms = jnp.concatenate([pos_coef[:, None] * query_rows, grad_neg], axis=0)
    rhs_grad = add_rows(both_tables, both_terms)
    return (lhs_grad, rhs_grad)


def per_device(
    embeddings,
    adagrad_state,
    relation_diag,
    bucket_counts,
    src_index,
    dst_index,
    rel_index,
    neg_index,
):
    emb_half = embeddings.astype(jnp.bfloat16)
    quarter = emb_half.shape[0]
    n_group = lax.axis_size("group")
    part_rows = n_group * quarter
    g = lax.axis_index("group")
    odd = (lax.axis_index("dom") % 2) == 1

    def local_rows(ids):
        return ((g - ids // quarter) % n_group) * quarter + ids % quarter

    edge_slots = src_index.shape[2]
    slot_ids = g * edge_slots + lax.iota(jnp.int32, edge_slots)

    other2 = parity_swap(emb_half, "dom", 2)
    far1 = from_behind(emb_half, "dom", 1)
    first = group_gather(jnp.stack([emb_half, other2]))
    own_block = first[0]
    other_block2 = first[1]
    rhs_block1 = group_gather(far1[None])[0]

    ids2 = jnp.stack(
        [src_index[1, 0], dst_index[1, 0], rel_index[1, 0], neg_index[1, 0, 0],
         jnp.broadcast_to(bucket_counts[1, 0], (edge_slots,))]
    )
    ids2_far = from_behind(ids2, "dom", -2)
    ids2 = jnp.where(odd, ids2_far, ids2)

    live2 = (slot_ids < ids2[4]).astype(jnp.float32)
    lhs_block2 = jnp.where(odd, other_block2, own_block)
    rhs_block2 = jnp.where(odd, own_block, other_block2)
    lhs_grad2, rhs_grad2 = block_grads(
        lhs_block2,
        rhs_block2,
        relation_diag,
        local_rows(ids2[0]),
        local_rows(ids2[1]),
        ids2[2],
        local_rows(ids2[3]),
        live2,
    )
    keep2 = jnp.where(odd, rhs_grad2, lhs_grad2)
    send2 = jnp.where(odd, lhs_grad2, rhs_grad2)
    recv2 = parity_return(send2, "dom", 2)

    live1 = (slot_ids < bucket_counts[0, 0]).astype(jnp.float32)
    lhs_grad1, rhs_grad1 = block_grads(
        own_block,
        rhs_block1,
        relation_diag,
        local_rows(src_index[0, 0]),
        local_rows(dst_index[0, 0]),
        rel_index[0, 0],
        local_rows(neg_index[0, 0, 0]),
        live1,
    )
    recv1 = from_behind(rhs_grad1, "dom", -1)

    stacked_total = lhs_grad1 + keep2 + recv1 + recv2
    grad_total = group_reduce_scatter(stacked_total, quarter)
    new_state = adagrad_state + jnp.mean(grad_total * grad_total, axis=1)
    new_embeddings = embeddings - LEARN_RATE * grad_total / (jnp.sqrt(new_state)[:, None] + ROW_EPS)
    return (new_embeddings, new_state)


def solution(mesh):
    placed = (
        P(("dom", "group"), None),
        P(("dom", "group")),
        P(),
        P(None, "dom"),
        P(None, "dom", "group"),
        P(None, "dom", "group"),
        P(None, "dom", "group"),
        P(None, "dom", "group", None),
    )
    return jax.shard_map(
        per_device,
        mesh=mesh,
        in_specs=placed,
        out_specs=(P(("dom", "group"), None), P(("dom", "group"))),
        check_vma=False,
    )
```

```python
import jax
import jax.numpy as jnp
from jax import lax
from jax.sharding import PartitionSpec as P

ROUNDS = 2


LEARN_RATE = 0.1
ROW_EPS = 1e-06


def from_behind(block, axis, distance):
    devices = range(lax.axis_size(axis))
    route = [((i - distance) % len(devices), i) for i in devices]
    return lax.ppermute(block, axis, route)


def parity_swap(block, axis, distance):
    n = lax.axis_size(axis)
    route = [((i - distance) % n, i) if i % 2 == 0 else ((i + distance) % n, i) for i in range(n)]
    return lax.ppermute(block, axis, route)


def parity_return(block, axis, distance):
    n = lax.axis_size(axis)
    route = [(i, (i - distance) % n) if i % 2 == 0 else (i, (i + distance) % n) for i in range(n)]
    return lax.ppermute(block, axis, route)


def group_gather(x):
    half = x.shape[1] // 2
    p1 = from_behind(x, "group", 1)
    p3 = from_behind(x, "group", -1)
    p2a = from_behind(p1[:, :half], "group", 1)
    p2b = from_behind(p3[:, half:], "group", -1)
    return jnp.concatenate([x, p1, p2a, p2b, p3], axis=1)


def group_reduce_scatter(y, quarter):
    half = quarter // 2
    c0, c1, c2, c3 = (y[s * quarter:(s + 1) * quarter] for s in range(4))
    plus1 = from_behind(jnp.concatenate([c2[:half], c3[half:]]), "group", 1)
    minus1 = from_behind(jnp.concatenate([c2[half:], c1[:half]]), "group", -1)
    plus2 = from_behind(plus1[:half] + c3[:half], "group", 1)
    minus2 = from_behind(minus1[:half] + c1[half:], "group", -1)
    top = c0[:half] + plus2 + minus1[half:]
    bottom = c0[half:] + plus1[half:] + minus2
    return jnp.concatenate([top, bottom], axis=0)


def select_table(row_ids, count):
    return row_ids[:, None] == lax.iota(jnp.int32, count)[None, :]


def pick_rows(table, block):
    return jnp.dot(table.astype(jnp.bfloat16), block, preferred_element_type=jnp.float32).astype(
        jnp.bfloat16
    )


def add_rows(table, values):
    hi_wide = lax.reduce_precision(values, exponent_bits=8, mantissa_bits=7)
    hi = hi_wide.astype(jnp.bfloat16)
    lo = (values - hi_wide).astype(jnp.bfloat16)
    both = jnp.concatenate([hi, lo], axis=1)
    summed = lax.dot_general(
        table.astype(jnp.bfloat16), both, (((0,), (0,)), ((), ())), preferred_element_type=jnp.float32
    )
    width = values.shape[1]
    return summed[:, :width] + summed[:, width:]


def block_grads(lhs_block, rhs_block, relation_diag, src_ids, dst_ids, rel_ids, neg_ids, live_mask):
    part_rows = lhs_block.shape[0]
    src_table = select_table(src_ids, part_rows)
    dst_table = select_table(dst_ids, part_rows)
    neg_table = select_table(neg_ids, part_rows)
    lhs_rows = pick_rows(src_table, lhs_block)
    rhs_rows = pick_rows(dst_table, rhs_block)
    neg_rows = pick_rows(neg_table, rhs_block)
    relation_count = relation_diag.shape[0]
    onehot = select_table(rel_ids, relation_count).astype(jnp.float32)
    rel_rows = jnp.dot(onehot, relation_diag, precision=lax.Precision.HIGHEST)
    query_rows = lhs_rows.astype(jnp.float32) * rel_rows
    query_half = query_rows.astype(jnp.bfloat16)
    rhs_wide = rhs_rows.astype(jnp.float32)
    pos_score = jnp.sum(query_rows * rhs_wide, axis=1)
    scores = lax.dot_general(
        query_half, neg_rows, (((1,), (1,)), ((), ())), preferred_element_type=jnp.float32
    )
    weights = (live_mask[:, None] * jax.nn.sigmoid(scores) / neg_ids.shape[0]).astype(jnp.bfloat16)
    pos_coef = -live_mask * jax.nn.sigmoid(-pos_score)
    grad_query = pos_coef[:, None] * rhs_wide + jnp.dot(
        weights, neg_rows, preferred_element_type=jnp.float32
    )
    grad_neg = lax.dot_general(
        weights, query_half, (((0,), (0,)), ((), ())), preferred_element_type=jnp.float32
    )
    lhs_grad = add_rows(src_table, grad_query * rel_rows)
    both_tables = jnp.concatenate([dst_table, neg_table], axis=0)
    both_terms = jnp.concatenate([pos_coef[:, None] * query_rows, grad_neg], axis=0)
    rhs_grad = add_rows(both_tables, both_terms)
    return (lhs_grad, rhs_grad)


def per_device(
    embeddings,
    adagrad_state,
    relation_diag,
    bucket_counts,
    src_index,
    dst_index,
    rel_index,
    neg_index,
):
    emb_half = embeddings.astype(jnp.bfloat16)
    quarter = emb_half.shape[0]
    n_group = lax.axis_size("group")
    part_rows = n_group * quarter
    g = lax.axis_index("group")
    odd = (lax.axis_index("dom") % 2) == 1

    def local_rows(ids):
        return ((g - ids // quarter) % n_group) * quarter + ids % quarter

    edge_slots = src_index.shape[2]
    slot_ids = g * edge_slots + lax.iota(jnp.int32, edge_slots)

    own_block = group_gather(emb_half[None])[0]
    other2 = parity_swap(emb_half, "dom", 2)
    far1 = from_behind(emb_half, "dom", 1)
    fetched = group_gather(jnp.stack([other2, far1]))
    other_block2 = fetched[0]
    rhs_block1 = fetched[1]

    ids2 = jnp.stack(
        [src_index[1, 0], dst_index[1, 0], rel_index[1, 0], neg_index[1, 0, 0],
         jnp.broadcast_to(bucket_counts[1, 0], (edge_slots,))]
    )
    ids2_far = from_behind(ids2, "dom", -2)
    ids2 = jnp.where(odd, ids2_far, ids2)

    live2 = (slot_ids < ids2[4]).astype(jnp.float32)
    lhs_block2 = jnp.where(odd, other_block2, own_block)
    rhs_block2 = jnp.where(odd, own_block, other_block2)
    lhs_grad2, rhs_grad2 = block_grads(
        lhs_block2,
        rhs_block2,
        relation_diag,
        local_rows(ids2[0]),
        local_rows(ids2[1]),
        ids2[2],
        local_rows(ids2[3]),
        live2,
    )
    keep2 = jnp.where(odd, rhs_grad2, lhs_grad2)
    send2 = jnp.where(odd, lhs_grad2, rhs_grad2)
    recv2 = parity_return(send2.astype(jnp.bfloat16), "dom", 2).astype(jnp.float32)

    live1 = (slot_ids < bucket_counts[0, 0]).astype(jnp.float32)
    lhs_grad1, rhs_grad1 = block_grads(
        own_block,
        rhs_block1,
        relation_diag,
        local_rows(src_index[0, 0]),
        local_rows(dst_index[0, 0]),
        rel_index[0, 0],
        local_rows(neg_index[0, 0, 0]),
        live1,
    )
    recv1 = from_behind(rhs_grad1.astype(jnp.bfloat16), "dom", -1).astype(jnp.float32)

    stacked_total = lhs_grad1 + keep2 + recv1 + recv2
    grad_total = group_reduce_scatter(stacked_total, quarter)
    new_state = adagrad_state + jnp.mean(grad_total * grad_total, axis=1)
    new_embeddings = embeddings - LEARN_RATE * grad_total / (jnp.sqrt(new_state)[:, None] + ROW_EPS)
    return (new_embeddings, new_state)


def solution(mesh):
    placed = (
        P(("dom", "group"), None),
        P(("dom", "group")),
        P(),
        P(None, "dom"),
        P(None, "dom", "group"),
        P(None, "dom", "group"),
        P(None, "dom", "group"),
        P(None, "dom", "group", None),
    )
    return jax.shard_map(
        per_device,
        mesh=mesh,
        in_specs=placed,
        out_specs=(P(("dom", "group"), None), P(("dom", "group"))),
        check_vma=False,
    )
```

```python
import jax
import jax.numpy as jnp
from jax import lax
from jax.sharding import PartitionSpec as P

ROUNDS = 2


LEARN_RATE = 0.1
ROW_EPS = 1e-06


def from_behind(block, axis, distance):
    devices = range(lax.axis_size(axis))
    route = [((i - distance) % len(devices), i) for i in devices]
    return lax.ppermute(block, axis, route)


def parity_swap(block, axis, distance):
    n = lax.axis_size(axis)
    route = [((i - distance) % n, i) if i % 2 == 0 else ((i + distance) % n, i) for i in range(n)]
    return lax.ppermute(block, axis, route)


def parity_return(block, axis, distance):
    n = lax.axis_size(axis)
    route = [(i, (i - distance) % n) if i % 2 == 0 else (i, (i + distance) % n) for i in range(n)]
    return lax.ppermute(block, axis, route)


def group_gather(x):
    half = x.shape[1] // 2
    p1 = from_behind(x, "group", 1)
    p3 = from_behind(x, "group", -1)
    p2a = from_behind(p1[:, :half], "group", 1)
    p2b = from_behind(p3[:, half:], "group", -1)
    return jnp.concatenate([x, p1, p2a, p2b, p3], axis=1)


def group_reduce_scatter(y, quarter):
    half = quarter // 2
    c0, c1, c2, c3 = (y[s * quarter:(s + 1) * quarter] for s in range(4))
    plus_src, minus_src = lax.optimization_barrier(
        (jnp.concatenate([c2[:half], c3[half:]]), jnp.concatenate([c2[half:], c1[:half]]))
    )
    plus1 = from_behind(plus_src, "group", 1)
    minus1 = from_behind(minus_src, "group", -1)
    plus_next, minus_next, top, bottom = lax.optimization_barrier(
        (plus1[:half] + c3[:half], minus1[:half] + c1[half:],
         c0[:half] + minus1[half:], c0[half:] + plus1[half:])
    )
    plus2 = from_behind(plus_next, "group", 1)
    minus2 = from_behind(minus_next, "group", -1)
    top = top + plus2
    bottom = bottom + minus2
    return jnp.concatenate([top, bottom], axis=0)


def select_table(row_ids, count):
    return row_ids[:, None] == lax.iota(jnp.int32, count)[None, :]


def pick_rows(table, block):
    return jnp.dot(table.astype(jnp.bfloat16), block, preferred_element_type=jnp.float32).astype(
        jnp.bfloat16
    )


def add_rows(table, values):
    hi_wide = lax.reduce_precision(values, exponent_bits=8, mantissa_bits=7)
    hi = hi_wide.astype(jnp.bfloat16)
    lo = (values - hi_wide).astype(jnp.bfloat16)
    both = jnp.concatenate([hi, lo], axis=1)
    summed = lax.dot_general(
        table.astype(jnp.bfloat16), both, (((0,), (0,)), ((), ())), preferred_element_type=jnp.float32
    )
    width = values.shape[1]
    return summed[:, :width] + summed[:, width:]


def block_grads(lhs_block, rhs_block, relation_diag, src_ids, dst_ids, rel_ids, neg_ids, live_mask):
    part_rows = lhs_block.shape[0]
    src_table = select_table(src_ids, part_rows)
    dst_table = select_table(dst_ids, part_rows)
    neg_table = select_table(neg_ids, part_rows)
    lhs_rows = pick_rows(src_table, lhs_block)
    rhs_rows = pick_rows(dst_table, rhs_block)
    neg_rows = pick_rows(neg_table, rhs_block)
    relation_count = relation_diag.shape[0]
    onehot = select_table(rel_ids, relation_count).astype(jnp.float32)
    rel_rows = jnp.dot(onehot, relation_diag, precision=lax.Precision.HIGHEST)
    query_rows = lhs_rows.astype(jnp.float32) * rel_rows
    query_half = query_rows.astype(jnp.bfloat16)
    rhs_wide = rhs_rows.astype(jnp.float32)
    pos_score = jnp.sum(query_rows * rhs_wide, axis=1)
    scores = lax.dot_general(
        query_half, neg_rows, (((1,), (1,)), ((), ())), preferred_element_type=jnp.float32
    )
    weights = (live_mask[:, None] * jax.nn.sigmoid(scores) / neg_ids.shape[0]).astype(jnp.bfloat16)
    pos_coef = -live_mask * jax.nn.sigmoid(-pos_score)
    grad_query = pos_coef[:, None] * rhs_wide + jnp.dot(
        weights, neg_rows, preferred_element_type=jnp.float32
    )
    grad_neg = lax.dot_general(
        weights, query_half, (((0,), (0,)), ((), ())), preferred_element_type=jnp.float32
    )
    lhs_grad = add_rows(src_table, grad_query * rel_rows)
    both_tables = jnp.concatenate([dst_table, neg_table], axis=0)
    both_terms = jnp.concatenate([pos_coef[:, None] * query_rows, grad_neg], axis=0)
    rhs_grad = add_rows(both_tables, both_terms)
    return (lhs_grad, rhs_grad)


def per_device(
    embeddings,
    adagrad_state,
    relation_diag,
    bucket_counts,
    src_index,
    dst_index,
    rel_index,
    neg_index,
):
    emb_half = embeddings.astype(jnp.bfloat16)
    quarter = emb_half.shape[0]
    n_group = lax.axis_size("group")
    part_rows = n_group * quarter
    g = lax.axis_index("group")
    odd = (lax.axis_index("dom") % 2) == 1

    def local_rows(ids):
        return ((g - ids // quarter) % n_group) * quarter + ids % quarter

    edge_slots = src_index.shape[2]
    slot_ids = g * edge_slots + lax.iota(jnp.int32, edge_slots)

    own_block = group_gather(emb_half[None])[0]
    other2 = parity_swap(emb_half, "dom", 2)
    far1 = from_behind(emb_half, "dom", 1)
    fetched = group_gather(jnp.stack([other2, far1]))
    other_block2 = fetched[0]
    rhs_block1 = fetched[1]

    ids2 = jnp.stack(
        [src_index[1, 0], dst_index[1, 0], rel_index[1, 0], neg_index[1, 0, 0],
         jnp.broadcast_to(bucket_counts[1, 0], (edge_slots,))]
    )
    ids2_far = from_behind(ids2, "dom", -2)
    ids2 = jnp.where(odd, ids2_far, ids2)

    live2 = (slot_ids < ids2[4]).astype(jnp.float32)
    lhs_block2 = jnp.where(odd, other_block2, own_block)
    rhs_block2 = jnp.where(odd, own_block, other_block2)
    lhs_grad2, rhs_grad2 = block_grads(
        lhs_block2,
        rhs_block2,
        relation_diag,
        local_rows(ids2[0]),
        local_rows(ids2[1]),
        ids2[2],
        local_rows(ids2[3]),
        live2,
    )
    keep2 = jnp.where(odd, rhs_grad2, lhs_grad2)
    send2 = jnp.where(odd, lhs_grad2, rhs_grad2)
    recv2 = parity_return(send2.astype(jnp.bfloat16), "dom", 2).astype(jnp.float32)

    live1 = (slot_ids < bucket_counts[0, 0]).astype(jnp.float32)
    lhs_grad1, rhs_grad1 = block_grads(
        own_block,
        rhs_block1,
        relation_diag,
        local_rows(src_index[0, 0]),
        local_rows(dst_index[0, 0]),
        rel_index[0, 0],
        local_rows(neg_index[0, 0, 0]),
        live1,
    )
    recv1 = from_behind(rhs_grad1.astype(jnp.bfloat16), "dom", -1).astype(jnp.float32)

    stacked_total = lhs_grad1 + keep2 + recv1 + recv2
    grad_total = group_reduce_scatter(stacked_total, quarter)
    new_state = adagrad_state + jnp.mean(grad_total * grad_total, axis=1)
    new_embeddings = embeddings - LEARN_RATE * grad_total / (jnp.sqrt(new_state)[:, None] + ROW_EPS)
    return (new_embeddings, new_state)


def solution(mesh):
    placed = (
        P(("dom", "group"), None),
        P(("dom", "group")),
        P(),
        P(None, "dom"),
        P(None, "dom", "group"),
        P(None, "dom", "group"),
        P(None, "dom", "group"),
        P(None, "dom", "group", None),
    )
    return jax.shard_map(
        per_device,
        mesh=mesh,
        in_specs=placed,
        out_specs=(P(("dom", "group"), None), P(("dom", "group"))),
        check_vma=False,
    )
```

```python
import jax
import jax.numpy as jnp
from jax import lax
from jax.sharding import PartitionSpec as P

ROUNDS = 2


LEARN_RATE = 0.1
ROW_EPS = 1e-06


def from_behind(block, axis, distance):
    devices = range(lax.axis_size(axis))
    route = [((i - distance) % len(devices), i) for i in devices]
    return lax.ppermute(block, axis, route)


def parity_swap(block, axis, distance):
    n = lax.axis_size(axis)
    route = [((i - distance) % n, i) if i % 2 == 0 else ((i + distance) % n, i) for i in range(n)]
    return lax.ppermute(block, axis, route)


def parity_return(block, axis, distance):
    n = lax.axis_size(axis)
    route = [(i, (i - distance) % n) if i % 2 == 0 else (i, (i + distance) % n) for i in range(n)]
    return lax.ppermute(block, axis, route)


def group_gather(x):
    half = x.shape[1] // 2
    p1 = from_behind(x, "group", 1)
    p3 = from_behind(x, "group", -1)
    p2a = from_behind(p1[:, :half], "group", 1)
    p2b = from_behind(p3[:, half:], "group", -1)
    return jnp.concatenate([x, p1, p2a, p2b, p3], axis=1)


def group_reduce_scatter(y, quarter):
    half = quarter // 2
    c0, c1, c2, c3 = (y[s * quarter:(s + 1) * quarter] for s in range(4))
    plus_src, minus_src = lax.optimization_barrier(
        (jnp.concatenate([c2[:half], c3[half:]]), jnp.concatenate([c2[half:], c1[:half]]))
    )
    plus1 = from_behind(plus_src.astype(jnp.bfloat16), "group", 1).astype(jnp.float32)
    minus1 = from_behind(minus_src.astype(jnp.bfloat16), "group", -1).astype(jnp.float32)
    plus_next, minus_next, top, bottom = lax.optimization_barrier(
        (plus1[:half] + c3[:half], minus1[:half] + c1[half:],
         c0[:half] + minus1[half:], c0[half:] + plus1[half:])
    )
    plus2 = from_behind(plus_next.astype(jnp.bfloat16), "group", 1).astype(jnp.float32)
    minus2 = from_behind(minus_next.astype(jnp.bfloat16), "group", -1).astype(jnp.float32)
    top = top + plus2
    bottom = bottom + minus2
    return jnp.concatenate([top, bottom], axis=0)


def select_table(row_ids, count):
    return row_ids[:, None] == lax.iota(jnp.int32, count)[None, :]


def pick_rows(table, block):
    return jnp.dot(table.astype(jnp.bfloat16), block, preferred_element_type=jnp.float32).astype(
        jnp.bfloat16
    )


def add_rows(table, values):
    hi_wide = lax.reduce_precision(values, exponent_bits=8, mantissa_bits=7)
    hi = hi_wide.astype(jnp.bfloat16)
    lo = (values - hi_wide).astype(jnp.bfloat16)
    both = jnp.concatenate([hi, lo], axis=1)
    summed = lax.dot_general(
        table.astype(jnp.bfloat16), both, (((0,), (0,)), ((), ())), preferred_element_type=jnp.float32
    )
    width = values.shape[1]
    return summed[:, :width] + summed[:, width:]


def block_grads(lhs_block, rhs_block, relation_diag, src_ids, dst_ids, rel_ids, neg_ids, live_mask):
    part_rows = lhs_block.shape[0]
    src_table = select_table(src_ids, part_rows)
    dst_table = select_table(dst_ids, part_rows)
    neg_table = select_table(neg_ids, part_rows)
    lhs_rows = pick_rows(src_table, lhs_block)
    rhs_rows = pick_rows(dst_table, rhs_block)
    neg_rows = pick_rows(neg_table, rhs_block)
    relation_count = relation_diag.shape[0]
    onehot = select_table(rel_ids, relation_count).astype(jnp.float32)
    rel_rows = jnp.dot(onehot, relation_diag, precision=lax.Precision.HIGHEST)
    query_rows = lhs_rows.astype(jnp.float32) * rel_rows
    query_half = query_rows.astype(jnp.bfloat16)
    rhs_wide = rhs_rows.astype(jnp.float32)
    pos_score = jnp.sum(query_rows * rhs_wide, axis=1)
    scores = lax.dot_general(
        query_half, neg_rows, (((1,), (1,)), ((), ())), preferred_element_type=jnp.float32
    )
    weights = (live_mask[:, None] * jax.nn.sigmoid(scores) / neg_ids.shape[0]).astype(jnp.bfloat16)
    pos_coef = -live_mask * jax.nn.sigmoid(-pos_score)
    grad_query = pos_coef[:, None] * rhs_wide + jnp.dot(
        weights, neg_rows, preferred_element_type=jnp.float32
    )
    grad_neg = lax.dot_general(
        weights, query_half, (((0,), (0,)), ((), ())), preferred_element_type=jnp.float32
    )
    lhs_grad = add_rows(src_table, grad_query * rel_rows)
    both_tables = jnp.concatenate([dst_table, neg_table], axis=0)
    both_terms = jnp.concatenate([pos_coef[:, None] * query_rows, grad_neg], axis=0)
    rhs_grad = add_rows(both_tables, both_terms)
    return (lhs_grad, rhs_grad)


def per_device(
    embeddings,
    adagrad_state,
    relation_diag,
    bucket_counts,
    src_index,
    dst_index,
    rel_index,
    neg_index,
):
    emb_half = embeddings.astype(jnp.bfloat16)
    quarter = emb_half.shape[0]
    n_group = lax.axis_size("group")
    part_rows = n_group * quarter
    g = lax.axis_index("group")
    odd = (lax.axis_index("dom") % 2) == 1

    def local_rows(ids):
        return ((g - ids // quarter) % n_group) * quarter + ids % quarter

    edge_slots = src_index.shape[2]
    slot_ids = g * edge_slots + lax.iota(jnp.int32, edge_slots)

    own_block = group_gather(emb_half[None])[0]
    other2 = parity_swap(emb_half, "dom", 2)
    other_block2 = group_gather(other2[None])[0]
    rhs_block1 = from_behind(own_block, "dom", 1)

    ids2 = jnp.stack(
        [src_index[1, 0], dst_index[1, 0], rel_index[1, 0], neg_index[1, 0, 0],
         jnp.broadcast_to(bucket_counts[1, 0], (edge_slots,))]
    )
    ids2_far = from_behind(ids2, "dom", -2)
    ids2 = jnp.where(odd, ids2_far, ids2)

    live2 = (slot_ids < ids2[4]).astype(jnp.float32)
    lhs_block2 = jnp.where(odd, other_block2, own_block)
    rhs_block2 = jnp.where(odd, own_block, other_block2)
    lhs_grad2, rhs_grad2 = block_grads(
        lhs_block2,
        rhs_block2,
        relation_diag,
        local_rows(ids2[0]),
        local_rows(ids2[1]),
        ids2[2],
        local_rows(ids2[3]),
        live2,
    )
    keep2 = jnp.where(odd, rhs_grad2, lhs_grad2)
    send2 = jnp.where(odd, lhs_grad2, rhs_grad2)
    recv2 = parity_return(send2.astype(jnp.bfloat16), "dom", 2).astype(jnp.float32)

    live1 = (slot_ids < bucket_counts[0, 0]).astype(jnp.float32)
    lhs_grad1, rhs_grad1 = block_grads(
        own_block,
        rhs_block1,
        relation_diag,
        local_rows(src_index[0, 0]),
        local_rows(dst_index[0, 0]),
        rel_index[0, 0],
        local_rows(neg_index[0, 0, 0]),
        live1,
    )
    recv1 = from_behind(rhs_grad1.astype(jnp.bfloat16), "dom", -1).astype(jnp.float32)

    stacked_total = lhs_grad1 + keep2 + recv1 + recv2
    grad_total = group_reduce_scatter(stacked_total, quarter)
    new_state = adagrad_state + jnp.mean(grad_total * grad_total, axis=1)
    new_embeddings = embeddings - LEARN_RATE * grad_total / (jnp.sqrt(new_state)[:, None] + ROW_EPS)
    return (new_embeddings, new_state)


def solution(mesh):
    placed = (
        P(("dom", "group"), None),
        P(("dom", "group")),
        P(),
        P(None, "dom"),
        P(None, "dom", "group"),
        P(None, "dom", "group"),
        P(None, "dom", "group"),
        P(None, "dom", "group", None),
    )
    return jax.shard_map(
        per_device,
        mesh=mesh,
        in_specs=placed,
        out_specs=(P(("dom", "group"), None), P(("dom", "group"))),
        check_vma=False,
    )
```

```python
import jax
import jax.numpy as jnp
from jax import lax
from jax.sharding import PartitionSpec as P

ROUNDS = 2


LEARN_RATE = 0.1
ROW_EPS = 1e-06


def from_behind(block, axis, distance):
    devices = range(lax.axis_size(axis))
    route = [((i - distance) % len(devices), i) for i in devices]
    return lax.ppermute(block, axis, route)


def parity_swap(block, axis, distance):
    n = lax.axis_size(axis)
    route = [((i - distance) % n, i) if i % 2 == 0 else ((i + distance) % n, i) for i in range(n)]
    return lax.ppermute(block, axis, route)


def parity_return(block, axis, distance):
    n = lax.axis_size(axis)
    route = [(i, (i - distance) % n) if i % 2 == 0 else (i, (i + distance) % n) for i in range(n)]
    return lax.ppermute(block, axis, route)


def group_gather(x):
    half = x.shape[1] // 2
    p1 = from_behind(x, "group", 1)
    p3 = from_behind(x, "group", -1)
    p2a = from_behind(p1[:, :half], "group", 1)
    p2b = from_behind(p3[:, half:], "group", -1)
    return jnp.concatenate([x, p1, p2a, p2b, p3], axis=1)


def group_reduce_scatter(y, quarter):
    half = quarter // 2
    c0, c1, c2, c3 = (y[s * quarter:(s + 1) * quarter] for s in range(4))
    plus_src, minus_src = lax.optimization_barrier(
        (jnp.concatenate([c2[:half], c3[half:]]), jnp.concatenate([c2[half:], c1[:half]]))
    )
    plus1 = from_behind(plus_src.astype(jnp.bfloat16), "group", 1).astype(jnp.float32)
    minus1 = from_behind(minus_src.astype(jnp.bfloat16), "group", -1).astype(jnp.float32)
    plus_next, minus_next, top, bottom = lax.optimization_barrier(
        (plus1[:half] + c3[:half], minus1[:half] + c1[half:],
         c0[:half] + minus1[half:], c0[half:] + plus1[half:])
    )
    plus2 = from_behind(plus_next.astype(jnp.bfloat16), "group", 1).astype(jnp.float32)
    minus2 = from_behind(minus_next.astype(jnp.bfloat16), "group", -1).astype(jnp.float32)
    top = top + plus2
    bottom = bottom + minus2
    return jnp.concatenate([top, bottom], axis=0)


def select_table(row_ids, count):
    return row_ids[:, None] == lax.iota(jnp.int32, count)[None, :]


def pick_rows(table, block):
    return jnp.dot(table.astype(jnp.bfloat16), block, preferred_element_type=jnp.float32).astype(
        jnp.bfloat16
    )


def add_rows(table, values):
    return lax.dot_general(
        table.astype(jnp.bfloat16),
        values.astype(jnp.bfloat16),
        (((0,), (0,)), ((), ())),
        preferred_element_type=jnp.float32,
    )


def block_grads(lhs_block, rhs_block, relation_diag, src_ids, dst_ids, rel_ids, neg_ids, live_mask):
    part_rows = lhs_block.shape[0]
    src_table = select_table(src_ids, part_rows)
    dst_table = select_table(dst_ids, part_rows)
    neg_table = select_table(neg_ids, part_rows)
    lhs_rows = pick_rows(src_table, lhs_block)
    rhs_rows = pick_rows(dst_table, rhs_block)
    neg_rows = pick_rows(neg_table, rhs_block)
    relation_count = relation_diag.shape[0]
    onehot = select_table(rel_ids, relation_count).astype(jnp.float32)
    rel_rows = jnp.dot(onehot, relation_diag, precision=lax.Precision.HIGHEST)
    query_rows = lhs_rows.astype(jnp.float32) * rel_rows
    query_half = query_rows.astype(jnp.bfloat16)
    rhs_wide = rhs_rows.astype(jnp.float32)
    pos_score = jnp.sum(query_rows * rhs_wide, axis=1)
    scores = lax.dot_general(
        query_half, neg_rows, (((1,), (1,)), ((), ())), preferred_element_type=jnp.float32
    )
    weights = (live_mask[:, None] * jax.nn.sigmoid(scores) / neg_ids.shape[0]).astype(jnp.bfloat16)
    pos_coef = -live_mask * jax.nn.sigmoid(-pos_score)
    grad_query = pos_coef[:, None] * rhs_wide + jnp.dot(
        weights, neg_rows, preferred_element_type=jnp.float32
    )
    grad_neg = lax.dot_general(
        weights, query_half, (((0,), (0,)), ((), ())), preferred_element_type=jnp.float32
    )
    lhs_grad = add_rows(src_table, grad_query * rel_rows)
    both_tables = jnp.concatenate([dst_table, neg_table], axis=0)
    both_terms = jnp.concatenate([pos_coef[:, None] * query_rows, grad_neg], axis=0)
    rhs_grad = add_rows(both_tables, both_terms)
    return (lhs_grad, rhs_grad)


def per_device(
    embeddings,
    adagrad_state,
    relation_diag,
    bucket_counts,
    src_index,
    dst_index,
    rel_index,
    neg_index,
):
    emb_half = embeddings.astype(jnp.bfloat16)
    quarter = emb_half.shape[0]
    n_group = lax.axis_size("group")
    part_rows = n_group * quarter
    g = lax.axis_index("group")
    odd = (lax.axis_index("dom") % 2) == 1

    def local_rows(ids):
        return ((g - ids // quarter) % n_group) * quarter + ids % quarter

    edge_slots = src_index.shape[2]
    slot_ids = g * edge_slots + lax.iota(jnp.int32, edge_slots)

    own_block = group_gather(emb_half[None])[0]
    other2 = parity_swap(emb_half, "dom", 2)
    other_block2 = group_gather(other2[None])[0]
    rhs_block1 = from_behind(own_block, "dom", 1)

    ids2 = jnp.stack(
        [src_index[1, 0], dst_index[1, 0], rel_index[1, 0], neg_index[1, 0, 0],
         jnp.broadcast_to(bucket_counts[1, 0], (edge_slots,))]
    )
    ids2_far = from_behind(ids2, "dom", -2)
    ids2 = jnp.where(odd, ids2_far, ids2)

    live2 = (slot_ids < ids2[4]).astype(jnp.float32)
    lhs_block2 = jnp.where(odd, other_block2, own_block)
    rhs_block2 = jnp.where(odd, own_block, other_block2)
    lhs_grad2, rhs_grad2 = block_grads(
        lhs_block2,
        rhs_block2,
        relation_diag,
        local_rows(ids2[0]),
        local_rows(ids2[1]),
        ids2[2],
        local_rows(ids2[3]),
        live2,
    )
    keep2 = jnp.where(odd, rhs_grad2, lhs_grad2)
    send2 = jnp.where(odd, lhs_grad2, rhs_grad2)
    recv2 = parity_return(send2.astype(jnp.bfloat16), "dom", 2).astype(jnp.float32)

    live1 = (slot_ids < bucket_counts[0, 0]).astype(jnp.float32)
    lhs_grad1, rhs_grad1 = block_grads(
        own_block,
        rhs_block1,
        relation_diag,
        local_rows(src_index[0, 0]),
        local_rows(dst_index[0, 0]),
        rel_index[0, 0],
        local_rows(neg_index[0, 0, 0]),
        live1,
    )
    recv1 = from_behind(rhs_grad1.astype(jnp.bfloat16), "dom", -1).astype(jnp.float32)

    stacked_total = lhs_grad1 + keep2 + recv1 + recv2
    grad_total = group_reduce_scatter(stacked_total, quarter)
    new_state = adagrad_state + jnp.mean(grad_total * grad_total, axis=1)
    new_embeddings = embeddings - LEARN_RATE * grad_total / (jnp.sqrt(new_state)[:, None] + ROW_EPS)
    return (new_embeddings, new_state)


def solution(mesh):
    placed = (
        P(("dom", "group"), None),
        P(("dom", "group")),
        P(),
        P(None, "dom"),
        P(None, "dom", "group"),
        P(None, "dom", "group"),
        P(None, "dom", "group"),
        P(None, "dom", "group", None),
    )
    return jax.shard_map(
        per_device,
        mesh=mesh,
        in_specs=placed,
        out_specs=(P(("dom", "group"), None), P(("dom", "group"))),
        check_vma=False,
    )
```

```python
import jax
import jax.numpy as jnp
from jax import lax
from jax.sharding import PartitionSpec as P

ROUNDS = 2


LEARN_RATE = 0.1
ROW_EPS = 1e-06


def from_behind(block, axis, distance):
    devices = range(lax.axis_size(axis))
    route = [((i - distance) % len(devices), i) for i in devices]
    return lax.ppermute(block, axis, route)


def parity_swap(block, axis, distance):
    n = lax.axis_size(axis)
    route = [((i - distance) % n, i) if i % 2 == 0 else ((i + distance) % n, i) for i in range(n)]
    return lax.ppermute(block, axis, route)


def parity_return(block, axis, distance):
    n = lax.axis_size(axis)
    route = [(i, (i - distance) % n) if i % 2 == 0 else (i, (i + distance) % n) for i in range(n)]
    return lax.ppermute(block, axis, route)


def group_gather(x):
    half = x.shape[1] // 2
    p1 = from_behind(x, "group", 1)
    p3 = from_behind(x, "group", -1)
    p2a = from_behind(p1[:, :half], "group", 1)
    p2b = from_behind(p3[:, half:], "group", -1)
    return jnp.concatenate([x, p1, p2a, p2b, p3], axis=1)


def group_reduce_scatter(y, quarter):
    n = lax.axis_size("group")
    g = lax.axis_index("group")
    chunks = y.reshape(n, quarter, y.shape[1])
    by_dest = jnp.take(chunks, (g - jnp.arange(n)) % n, axis=0)
    got = lax.all_to_all(by_dest.astype(jnp.bfloat16), "group", 0, 0, tiled=True)
    got = got.astype(jnp.float32)
    own = jnp.take(chunks, jnp.asarray([0]), axis=0)[0]
    mask = (jnp.arange(n) != g).astype(jnp.float32)[:, None, None]
    return own + jnp.sum(got * mask, axis=0)


def select_table(row_ids, count):
    return row_ids[:, None] == lax.iota(jnp.int32, count)[None, :]


def pick_rows(table, block):
    return jnp.dot(table.astype(jnp.bfloat16), block, preferred_element_type=jnp.float32).astype(
        jnp.bfloat16
    )


def add_rows(table, values):
    hi_wide = lax.reduce_precision(values, exponent_bits=8, mantissa_bits=7)
    hi = hi_wide.astype(jnp.bfloat16)
    lo = (values - hi_wide).astype(jnp.bfloat16)
    both = jnp.concatenate([hi, lo], axis=1)
    summed = lax.dot_general(
        table.astype(jnp.bfloat16), both, (((0,), (0,)), ((), ())), preferred_element_type=jnp.float32
    )
    width = values.shape[1]
    return summed[:, :width] + summed[:, width:]


def block_grads(lhs_block, rhs_block, relation_diag, src_ids, dst_ids, rel_ids, neg_ids, live_mask):
    part_rows = lhs_block.shape[0]
    src_table = select_table(src_ids, part_rows)
    dst_table = select_table(dst_ids, part_rows)
    neg_table = select_table(neg_ids, part_rows)
    lhs_rows = pick_rows(src_table, lhs_block)
    rhs_rows = pick_rows(dst_table, rhs_block)
    neg_rows = pick_rows(neg_table, rhs_block)
    relation_count = relation_diag.shape[0]
    onehot = select_table(rel_ids, relation_count).astype(jnp.float32)
    rel_rows = jnp.dot(onehot, relation_diag, precision=lax.Precision.HIGHEST)
    query_rows = lhs_rows.astype(jnp.float32) * rel_rows
    query_half = query_rows.astype(jnp.bfloat16)
    rhs_wide = rhs_rows.astype(jnp.float32)
    pos_score = jnp.sum(query_rows * rhs_wide, axis=1)
    scores = lax.dot_general(
        query_half, neg_rows, (((1,), (1,)), ((), ())), preferred_element_type=jnp.float32
    )
    weights = (live_mask[:, None] * jax.nn.sigmoid(scores) / neg_ids.shape[0]).astype(jnp.bfloat16)
    pos_coef = -live_mask * jax.nn.sigmoid(-pos_score)
    grad_query = pos_coef[:, None] * rhs_wide + jnp.dot(
        weights, neg_rows, preferred_element_type=jnp.float32
    )
    grad_neg = lax.dot_general(
        weights, query_half, (((0,), (0,)), ((), ())), preferred_element_type=jnp.float32
    )
    lhs_grad = add_rows(src_table, grad_query * rel_rows)
    both_tables = jnp.concatenate([dst_table, neg_table], axis=0)
    both_terms = jnp.concatenate([pos_coef[:, None] * query_rows, grad_neg], axis=0)
    rhs_grad = add_rows(both_tables, both_terms)
    return (lhs_grad, rhs_grad)


def per_device(
    embeddings,
    adagrad_state,
    relation_diag,
    bucket_counts,
    src_index,
    dst_index,
    rel_index,
    neg_index,
):
    emb_half = embeddings.astype(jnp.bfloat16)
    quarter = emb_half.shape[0]
    n_group = lax.axis_size("group")
    part_rows = n_group * quarter
    g = lax.axis_index("group")
    odd = (lax.axis_index("dom") % 2) == 1

    def local_rows(ids):
        return ((g - ids // quarter) % n_group) * quarter + ids % quarter

    edge_slots = src_index.shape[2]
    slot_ids = g * edge_slots + lax.iota(jnp.int32, edge_slots)

    own_block = group_gather(emb_half[None])[0]
    other2 = parity_swap(emb_half, "dom", 2)
    other_block2 = group_gather(other2[None])[0]
    rhs_block1 = from_behind(own_block, "dom", 1)

    ids2 = jnp.stack(
        [src_index[1, 0], dst_index[1, 0], rel_index[1, 0], neg_index[1, 0, 0],
         jnp.broadcast_to(bucket_counts[1, 0], (edge_slots,))]
    )
    ids2_far = from_behind(ids2, "dom", -2)
    ids2 = jnp.where(odd, ids2_far, ids2)

    live2 = (slot_ids < ids2[4]).astype(jnp.float32)
    lhs_block2 = jnp.where(odd, other_block2, own_block)
    rhs_block2 = jnp.where(odd, own_block, other_block2)
    lhs_grad2, rhs_grad2 = block_grads(
        lhs_block2,
        rhs_block2,
        relation_diag,
        local_rows(ids2[0]),
        local_rows(ids2[1]),
        ids2[2],
        local_rows(ids2[3]),
        live2,
    )
    keep2 = jnp.where(odd, rhs_grad2, lhs_grad2)
    send2 = jnp.where(odd, lhs_grad2, rhs_grad2)
    recv2 = parity_return(send2.astype(jnp.bfloat16), "dom", 2).astype(jnp.float32)

    live1 = (slot_ids < bucket_counts[0, 0]).astype(jnp.float32)
    lhs_grad1, rhs_grad1 = block_grads(
        own_block,
        rhs_block1,
        relation_diag,
        local_rows(src_index[0, 0]),
        local_rows(dst_index[0, 0]),
        rel_index[0, 0],
        local_rows(neg_index[0, 0, 0]),
        live1,
    )
    recv1 = from_behind(rhs_grad1.astype(jnp.bfloat16), "dom", -1).astype(jnp.float32)

    stacked_total = lhs_grad1 + keep2 + recv1 + recv2
    grad_total = group_reduce_scatter(stacked_total, quarter)
    new_state = adagrad_state + jnp.mean(grad_total * grad_total, axis=1)
    new_embeddings = embeddings - LEARN_RATE * grad_total / (jnp.sqrt(new_state)[:, None] + ROW_EPS)
    return (new_embeddings, new_state)


def solution(mesh):
    placed = (
        P(("dom", "group"), None),
        P(("dom", "group")),
        P(),
        P(None, "dom"),
        P(None, "dom", "group"),
        P(None, "dom", "group"),
        P(None, "dom", "group"),
        P(None, "dom", "group", None),
    )
    return jax.shard_map(
        per_device,
        mesh=mesh,
        in_specs=placed,
        out_specs=(P(("dom", "group"), None), P(("dom", "group"))),
        check_vma=False,
    )
```

```python
import jax
import jax.numpy as jnp
from jax import lax
from jax.sharding import PartitionSpec as P

ROUNDS = 2


LEARN_RATE = 0.1
ROW_EPS = 1e-06


def from_behind(block, axis, distance):
    devices = range(lax.axis_size(axis))
    route = [((i - distance) % len(devices), i) for i in devices]
    return lax.ppermute(block, axis, route)


def parity_swap(block, axis, distance):
    n = lax.axis_size(axis)
    route = [((i - distance) % n, i) if i % 2 == 0 else ((i + distance) % n, i) for i in range(n)]
    return lax.ppermute(block, axis, route)


def parity_return(block, axis, distance):
    n = lax.axis_size(axis)
    route = [(i, (i - distance) % n) if i % 2 == 0 else (i, (i + distance) % n) for i in range(n)]
    return lax.ppermute(block, axis, route)


def group_gather(x):
    half = x.shape[1] // 2
    p1 = from_behind(x, "group", 1)
    p3 = from_behind(x, "group", -1)
    p2a = from_behind(p1[:, :half], "group", 1)
    p2b = from_behind(p3[:, half:], "group", -1)
    return jnp.concatenate([x, p1, p2a, p2b, p3], axis=1)


def group_reduce_scatter(y, quarter):
    half = quarter // 2
    c0, c1, c2, c3 = (y[s * quarter:(s + 1) * quarter] for s in range(4))
    plus_src, minus_src = lax.optimization_barrier(
        (jnp.concatenate([c2[:half], c3[half:]]), jnp.concatenate([c2[half:], c1[:half]]))
    )
    plus1 = from_behind(plus_src.astype(jnp.bfloat16), "group", 1).astype(jnp.float32)
    minus1 = from_behind(minus_src.astype(jnp.bfloat16), "group", -1).astype(jnp.float32)
    plus_next, minus_next, top, bottom = lax.optimization_barrier(
        (plus1[:half] + c3[:half], minus1[:half] + c1[half:],
         c0[:half] + minus1[half:], c0[half:] + plus1[half:])
    )
    plus2 = from_behind(plus_next.astype(jnp.bfloat16), "group", 1).astype(jnp.float32)
    minus2 = from_behind(minus_next.astype(jnp.bfloat16), "group", -1).astype(jnp.float32)
    top = top + plus2
    bottom = bottom + minus2
    return jnp.concatenate([top, bottom], axis=0)


def select_table(row_ids, count):
    return row_ids[:, None] == lax.iota(jnp.int32, count)[None, :]


def pick_rows(table, block):
    return jnp.dot(table.astype(jnp.bfloat16), block, preferred_element_type=jnp.float32).astype(
        jnp.bfloat16
    )


def add_rows(table, values):
    hi_wide = lax.reduce_precision(values, exponent_bits=8, mantissa_bits=7)
    hi = hi_wide.astype(jnp.bfloat16)
    lo = (values - hi_wide).astype(jnp.bfloat16)
    both = jnp.concatenate([hi, lo], axis=1)
    summed = lax.dot_general(
        table.astype(jnp.bfloat16), both, (((0,), (0,)), ((), ())), preferred_element_type=jnp.float32
    )
    width = values.shape[1]
    return summed[:, :width] + summed[:, width:]


def block_grads(lhs_block, rhs_block, relation_diag, src_ids, dst_ids, rel_ids, neg_ids, live_mask,
                rhs_pieces=1):
    part_rows = lhs_block.shape[0]
    src_table = select_table(src_ids, part_rows)
    dst_table = select_table(dst_ids, part_rows)
    neg_table = select_table(neg_ids, part_rows)
    lhs_rows = pick_rows(src_table, lhs_block)
    rhs_rows = pick_rows(dst_table, rhs_block)
    neg_rows = pick_rows(neg_table, rhs_block)
    relation_count = relation_diag.shape[0]
    onehot = select_table(rel_ids, relation_count).astype(jnp.float32)
    rel_rows = jnp.dot(onehot, relation_diag, precision=lax.Precision.HIGHEST)
    query_rows = lhs_rows.astype(jnp.float32) * rel_rows
    query_half = query_rows.astype(jnp.bfloat16)
    rhs_wide = rhs_rows.astype(jnp.float32)
    pos_score = jnp.sum(query_rows * rhs_wide, axis=1)
    scores = lax.dot_general(
        query_half, neg_rows, (((1,), (1,)), ((), ())), preferred_element_type=jnp.float32
    )
    weights = (live_mask[:, None] * jax.nn.sigmoid(scores) / neg_ids.shape[0]).astype(jnp.bfloat16)
    pos_coef = -live_mask * jax.nn.sigmoid(-pos_score)
    grad_query = pos_coef[:, None] * rhs_wide + jnp.dot(
        weights, neg_rows, preferred_element_type=jnp.float32
    )
    grad_neg = lax.dot_general(
        weights, query_half, (((0,), (0,)), ((), ())), preferred_element_type=jnp.float32
    )
    both_tables = jnp.concatenate([dst_table, neg_table], axis=0)
    both_terms = jnp.concatenate([pos_coef[:, None] * query_rows, grad_neg], axis=0)
    piece = part_rows // rhs_pieces
    rhs_grad = [
        add_rows(both_tables[:, p * piece:(p + 1) * piece], both_terms) for p in range(rhs_pieces)
    ]
    lhs_grad = add_rows(src_table, grad_query * rel_rows)
    if rhs_pieces == 1:
        rhs_grad = rhs_grad[0]
    return (lhs_grad, rhs_grad)


def per_device(
    embeddings,
    adagrad_state,
    relation_diag,
    bucket_counts,
    src_index,
    dst_index,
    rel_index,
    neg_index,
):
    emb_half = embeddings.astype(jnp.bfloat16)
    quarter = emb_half.shape[0]
    n_group = lax.axis_size("group")
    part_rows = n_group * quarter
    g = lax.axis_index("group")
    odd = (lax.axis_index("dom") % 2) == 1

    def local_rows(ids):
        return ((g - ids // quarter) % n_group) * quarter + ids % quarter

    edge_slots = src_index.shape[2]
    slot_ids = g * edge_slots + lax.iota(jnp.int32, edge_slots)

    own_block = group_gather(emb_half[None])[0]
    other2 = parity_swap(emb_half, "dom", 2)
    other_block2 = group_gather(other2[None])[0]
    rhs_block1 = from_behind(own_block, "dom", 1)

    ids2 = jnp.stack(
        [src_index[1, 0], dst_index[1, 0], rel_index[1, 0], neg_index[1, 0, 0],
         jnp.broadcast_to(bucket_counts[1, 0], (edge_slots,))]
    )
    ids2_far = from_behind(ids2, "dom", -2)
    ids2 = jnp.where(odd, ids2_far, ids2)

    live2 = (slot_ids < ids2[4]).astype(jnp.float32)
    lhs_block2 = jnp.where(odd, other_block2, own_block)
    rhs_block2 = jnp.where(odd, own_block, other_block2)
    lhs_grad2, rhs_grad2 = block_grads(
        lhs_block2,
        rhs_block2,
        relation_diag,
        local_rows(ids2[0]),
        local_rows(ids2[1]),
        ids2[2],
        local_rows(ids2[3]),
        live2,
    )
    keep2 = jnp.where(odd, rhs_grad2, lhs_grad2)
    send2 = jnp.where(odd, lhs_grad2, rhs_grad2)
    recv2 = parity_return(send2.astype(jnp.bfloat16), "dom", 2).astype(jnp.float32)

    live1 = (slot_ids < bucket_counts[0, 0]).astype(jnp.float32)
    lhs_grad1, rhs_grad1 = block_grads(
        own_block,
        rhs_block1,
        relation_diag,
        local_rows(src_index[0, 0]),
        local_rows(dst_index[0, 0]),
        rel_index[0, 0],
        local_rows(neg_index[0, 0, 0]),
        live1,
        rhs_pieces=2,
    )
    recv1 = jnp.concatenate(
        [from_behind(p.astype(jnp.bfloat16), "dom", -1).astype(jnp.float32) for p in rhs_grad1]
    )

    stacked_total = lhs_grad1 + keep2 + recv1 + recv2
    grad_total = group_reduce_scatter(stacked_total, quarter)
    new_state = adagrad_state + jnp.mean(grad_total * grad_total, axis=1)
    new_embeddings = embeddings - LEARN_RATE * grad_total / (jnp.sqrt(new_state)[:, None] + ROW_EPS)
    return (new_embeddings, new_state)


def solution(mesh):
    placed = (
        P(("dom", "group"), None),
        P(("dom", "group")),
        P(),
        P(None, "dom"),
        P(None, "dom", "group"),
        P(None, "dom", "group"),
        P(None, "dom", "group"),
        P(None, "dom", "group", None),
    )
    return jax.shard_map(
        per_device,
        mesh=mesh,
        in_specs=placed,
        out_specs=(P(("dom", "group"), None), P(("dom", "group"))),
        check_vma=False,
    )
```

```python
import jax
import jax.numpy as jnp
from jax import lax
from jax.sharding import PartitionSpec as P

ROUNDS = 2


LEARN_RATE = 0.1
ROW_EPS = 1e-06


def from_behind(block, axis, distance):
    devices = range(lax.axis_size(axis))
    route = [((i - distance) % len(devices), i) for i in devices]
    return lax.ppermute(block, axis, route)


def parity_swap(block, axis, distance):
    n = lax.axis_size(axis)
    route = [((i - distance) % n, i) if i % 2 == 0 else ((i + distance) % n, i) for i in range(n)]
    return lax.ppermute(block, axis, route)


def parity_return(block, axis, distance):
    n = lax.axis_size(axis)
    route = [(i, (i - distance) % n) if i % 2 == 0 else (i, (i + distance) % n) for i in range(n)]
    return lax.ppermute(block, axis, route)


def group_gather(x):
    half = x.shape[1] // 2
    p1 = from_behind(x, "group", 1)
    p3 = from_behind(x, "group", -1)
    p2a = from_behind(p1[:, :half], "group", 1)
    p2b = from_behind(p3[:, half:], "group", -1)
    return jnp.concatenate([x, p1, p2a, p2b, p3], axis=1)


def group_gather_direct(x):
    p1 = from_behind(x, "group", 1)
    p2 = from_behind(x, "group", 2)
    p3 = from_behind(x, "group", -1)
    return jnp.concatenate([x, p1, p2, p3], axis=1)


def group_reduce_scatter(y, quarter):
    half = quarter // 2
    c0, c1, c2, c3 = (y[s * quarter:(s + 1) * quarter] for s in range(4))
    plus_src, minus_src = lax.optimization_barrier(
        (jnp.concatenate([c2[:half], c3[half:]]), jnp.concatenate([c2[half:], c1[:half]]))
    )
    plus1 = from_behind(plus_src.astype(jnp.bfloat16), "group", 1).astype(jnp.float32)
    minus1 = from_behind(minus_src.astype(jnp.bfloat16), "group", -1).astype(jnp.float32)
    plus_next, minus_next, top, bottom = lax.optimization_barrier(
        (plus1[:half] + c3[:half], minus1[:half] + c1[half:],
         c0[:half] + minus1[half:], c0[half:] + plus1[half:])
    )
    plus2 = from_behind(plus_next.astype(jnp.bfloat16), "group", 1).astype(jnp.float32)
    minus2 = from_behind(minus_next.astype(jnp.bfloat16), "group", -1).astype(jnp.float32)
    top = top + plus2
    bottom = bottom + minus2
    return jnp.concatenate([top, bottom], axis=0)


def select_table(row_ids, count):
    return row_ids[:, None] == lax.iota(jnp.int32, count)[None, :]


def pick_rows(table, block):
    return jnp.dot(table.astype(jnp.bfloat16), block, preferred_element_type=jnp.float32).astype(
        jnp.bfloat16
    )


def add_rows(table, values):
    hi_wide = lax.reduce_precision(values, exponent_bits=8, mantissa_bits=7)
    hi = hi_wide.astype(jnp.bfloat16)
    lo = (values - hi_wide).astype(jnp.bfloat16)
    both = jnp.concatenate([hi, lo], axis=1)
    summed = lax.dot_general(
        table.astype(jnp.bfloat16), both, (((0,), (0,)), ((), ())), preferred_element_type=jnp.float32
    )
    width = values.shape[1]
    return summed[:, :width] + summed[:, width:]


def block_grads(lhs_block, rhs_block, relation_diag, src_ids, dst_ids, rel_ids, neg_ids, live_mask):
    part_rows = lhs_block.shape[0]
    src_table = select_table(src_ids, part_rows)
    dst_table = select_table(dst_ids, part_rows)
    neg_table = select_table(neg_ids, part_rows)
    lhs_rows = pick_rows(src_table, lhs_block)
    rhs_rows = pick_rows(dst_table, rhs_block)
    neg_rows = pick_rows(neg_table, rhs_block)
    relation_count = relation_diag.shape[0]
    onehot = select_table(rel_ids, relation_count).astype(jnp.float32)
    rel_rows = jnp.dot(onehot, relation_diag, precision=lax.Precision.HIGHEST)
    query_rows = lhs_rows.astype(jnp.float32) * rel_rows
    query_half = query_rows.astype(jnp.bfloat16)
    rhs_wide = rhs_rows.astype(jnp.float32)
    pos_score = jnp.sum(query_rows * rhs_wide, axis=1)
    scores = lax.dot_general(
        query_half, neg_rows, (((1,), (1,)), ((), ())), preferred_element_type=jnp.float32
    )
    weights = (live_mask[:, None] * jax.nn.sigmoid(scores) / neg_ids.shape[0]).astype(jnp.bfloat16)
    pos_coef = -live_mask * jax.nn.sigmoid(-pos_score)
    grad_query = pos_coef[:, None] * rhs_wide + jnp.dot(
        weights, neg_rows, preferred_element_type=jnp.float32
    )
    grad_neg = lax.dot_general(
        weights, query_half, (((0,), (0,)), ((), ())), preferred_element_type=jnp.float32
    )
    lhs_grad = add_rows(src_table, grad_query * rel_rows)
    both_tables = jnp.concatenate([dst_table, neg_table], axis=0)
    both_terms = jnp.concatenate([pos_coef[:, None] * query_rows, grad_neg], axis=0)
    rhs_grad = add_rows(both_tables, both_terms)
    return (lhs_grad, rhs_grad)


def per_device(
    embeddings,
    adagrad_state,
    relation_diag,
    bucket_counts,
    src_index,
    dst_index,
    rel_index,
    neg_index,
):
    emb_half = embeddings.astype(jnp.bfloat16)
    quarter = emb_half.shape[0]
    n_group = lax.axis_size("group")
    part_rows = n_group * quarter
    g = lax.axis_index("group")
    odd = (lax.axis_index("dom") % 2) == 1

    def local_rows(ids):
        return ((g - ids // quarter) % n_group) * quarter + ids % quarter

    edge_slots = src_index.shape[2]
    slot_ids = g * edge_slots + lax.iota(jnp.int32, edge_slots)

    own_block = group_gather(emb_half[None])[0]
    other2 = parity_swap(emb_half, "dom", 2)
    other_block2 = group_gather_direct(other2[None])[0]
    rhs_block1 = from_behind(own_block, "dom", 1)

    ids2 = jnp.stack(
        [src_index[1, 0], dst_index[1, 0], rel_index[1, 0], neg_index[1, 0, 0],
         jnp.broadcast_to(bucket_counts[1, 0], (edge_slots,))]
    )
    ids2_far = from_behind(ids2, "dom", -2)
    ids2 = jnp.where(odd, ids2_far, ids2)

    live2 = (slot_ids < ids2[4]).astype(jnp.float32)
    lhs_block2 = jnp.where(odd, other_block2, own_block)
    rhs_block2 = jnp.where(odd, own_block, other_block2)
    lhs_grad2, rhs_grad2 = block_grads(
        lhs_block2,
        rhs_block2,
        relation_diag,
        local_rows(ids2[0]),
        local_rows(ids2[1]),
        ids2[2],
        local_rows(ids2[3]),
        live2,
    )
    keep2 = jnp.where(odd, rhs_grad2, lhs_grad2)
    send2 = jnp.where(odd, lhs_grad2, rhs_grad2)
    recv2 = parity_return(send2.astype(jnp.bfloat16), "dom", 2).astype(jnp.float32)

    live1 = (slot_ids < bucket_counts[0, 0]).astype(jnp.float32)
    lhs_grad1, rhs_grad1 = block_grads(
        own_block,
        rhs_block1,
        relation_diag,
        local_rows(src_index[0, 0]),
        local_rows(dst_index[0, 0]),
        rel_index[0, 0],
        local_rows(neg_index[0, 0, 0]),
        live1,
    )
    recv1 = from_behind(rhs_grad1.astype(jnp.bfloat16), "dom", -1).astype(jnp.float32)

    stacked_total = lhs_grad1 + keep2 + recv1 + recv2
    grad_total = group_reduce_scatter(stacked_total, quarter)
    new_state = adagrad_state + jnp.mean(grad_total * grad_total, axis=1)
    new_embeddings = embeddings - LEARN_RATE * grad_total / (jnp.sqrt(new_state)[:, None] + ROW_EPS)
    return (new_embeddings, new_state)


def solution(mesh):
    placed = (
        P(("dom", "group"), None),
        P(("dom", "group")),
        P(),
        P(None, "dom"),
        P(None, "dom", "group"),
        P(None, "dom", "group"),
        P(None, "dom", "group"),
        P(None, "dom", "group", None),
    )
    return jax.shard_map(
        per_device,
        mesh=mesh,
        in_specs=placed,
        out_specs=(P(("dom", "group"), None), P(("dom", "group"))),
        check_vma=False,
    )
```

```python
import jax
import jax.numpy as jnp
from jax import lax
from jax.sharding import PartitionSpec as P

ROUNDS = 2


LEARN_RATE = 0.1
ROW_EPS = 1e-06


def from_behind(block, axis, distance):
    devices = range(lax.axis_size(axis))
    route = [((i - distance) % len(devices), i) for i in devices]
    return lax.ppermute(block, axis, route)


def parity_swap(block, axis, distance):
    n = lax.axis_size(axis)
    route = [((i - distance) % n, i) if i % 2 == 0 else ((i + distance) % n, i) for i in range(n)]
    return lax.ppermute(block, axis, route)


def parity_return(block, axis, distance):
    n = lax.axis_size(axis)
    route = [(i, (i - distance) % n) if i % 2 == 0 else (i, (i + distance) % n) for i in range(n)]
    return lax.ppermute(block, axis, route)


def group_gather(x):
    half = x.shape[1] // 2
    p1 = from_behind(x, "group", 1)
    p3 = from_behind(x, "group", -1)
    p2a = from_behind(p1[:, :half], "group", 1)
    p2b = from_behind(p3[:, half:], "group", -1)
    return jnp.concatenate([x, p1, p2a, p2b, p3], axis=1)


def group_reduce_scatter(y, quarter):
    half = quarter // 2
    c0, c1, c2, c3 = (y[s * quarter:(s + 1) * quarter] for s in range(4))
    plus_src, minus_src = lax.optimization_barrier(
        (jnp.concatenate([c2[:half], c3[half:]]), jnp.concatenate([c2[half:], c1[:half]]))
    )
    plus1 = from_behind(plus_src.astype(jnp.bfloat16), "group", 1).astype(jnp.float32)
    minus1 = from_behind(minus_src.astype(jnp.bfloat16), "group", -1).astype(jnp.float32)
    plus_next, minus_next, top, bottom = lax.optimization_barrier(
        (plus1[:half] + c3[:half], minus1[:half] + c1[half:],
         c0[:half] + minus1[half:], c0[half:] + plus1[half:])
    )
    plus2 = from_behind(plus_next.astype(jnp.bfloat16), "group", 1).astype(jnp.float32)
    minus2 = from_behind(minus_next.astype(jnp.bfloat16), "group", -1).astype(jnp.float32)
    top = top + plus2
    bottom = bottom + minus2
    return jnp.concatenate([top, bottom], axis=0)


def select_table(row_ids, count):
    return row_ids[:, None] == lax.iota(jnp.int32, count)[None, :]


def pick_rows(table, block):
    return jnp.dot(table.astype(jnp.bfloat16), block, preferred_element_type=jnp.float32).astype(
        jnp.bfloat16
    )


def add_rows(table, values):
    hi_wide = lax.reduce_precision(values, exponent_bits=8, mantissa_bits=7)
    hi = hi_wide.astype(jnp.bfloat16)
    lo = (values - hi_wide).astype(jnp.bfloat16)
    table = table.astype(jnp.bfloat16)
    dims = (((0,), (0,)), ((), ()))
    return lax.dot_general(table, hi, dims, preferred_element_type=jnp.float32) + lax.dot_general(
        table, lo, dims, preferred_element_type=jnp.float32
    )


def block_grads(lhs_block, rhs_block, relation_diag, src_ids, dst_ids, rel_ids, neg_ids, live_mask):
    part_rows = lhs_block.shape[0]
    src_table = select_table(src_ids, part_rows)
    dst_table = select_table(dst_ids, part_rows)
    neg_table = select_table(neg_ids, part_rows)
    lhs_rows = pick_rows(src_table, lhs_block)
    rhs_rows = pick_rows(dst_table, rhs_block)
    neg_rows = pick_rows(neg_table, rhs_block)
    relation_count = relation_diag.shape[0]
    onehot = select_table(rel_ids, relation_count).astype(jnp.float32)
    rel_rows = jnp.dot(onehot, relation_diag, precision=lax.Precision.HIGHEST)
    query_rows = lhs_rows.astype(jnp.float32) * rel_rows
    query_half = query_rows.astype(jnp.bfloat16)
    rhs_wide = rhs_rows.astype(jnp.float32)
    pos_score = jnp.sum(query_rows * rhs_wide, axis=1)
    scores = lax.dot_general(
        query_half, neg_rows, (((1,), (1,)), ((), ())), preferred_element_type=jnp.float32
    )
    weights = (live_mask[:, None] * jax.nn.sigmoid(scores) / neg_ids.shape[0]).astype(jnp.bfloat16)
    pos_coef = -live_mask * jax.nn.sigmoid(-pos_score)
    grad_query = pos_coef[:, None] * rhs_wide + jnp.dot(
        weights, neg_rows, preferred_element_type=jnp.float32
    )
    grad_neg = lax.dot_general(
        weights, query_half, (((0,), (0,)), ((), ())), preferred_element_type=jnp.float32
    )
    lhs_grad = add_rows(src_table, grad_query * rel_rows)
    rhs_grad = add_rows(dst_table, pos_coef[:, None] * query_rows) + add_rows(neg_table, grad_neg)
    return (lhs_grad, rhs_grad)


def per_device(
    embeddings,
    adagrad_state,
    relation_diag,
    bucket_counts,
    src_index,
    dst_index,
    rel_index,
    neg_index,
):
    emb_half = embeddings.astype(jnp.bfloat16)
    quarter = emb_half.shape[0]
    n_group = lax.axis_size("group")
    part_rows = n_group * quarter
    g = lax.axis_index("group")
    odd = (lax.axis_index("dom") % 2) == 1

    def local_rows(ids):
        return ((g - ids // quarter) % n_group) * quarter + ids % quarter

    edge_slots = src_index.shape[2]
    slot_ids = g * edge_slots + lax.iota(jnp.int32, edge_slots)

    own_block = group_gather(emb_half[None])[0]
    other2 = parity_swap(emb_half, "dom", 2)
    other_block2 = group_gather(other2[None])[0]
    rhs_block1 = from_behind(own_block, "dom", 1)

    ids2 = jnp.stack(
        [src_index[1, 0], dst_index[1, 0], rel_index[1, 0], neg_index[1, 0, 0],
         jnp.broadcast_to(bucket_counts[1, 0], (edge_slots,))]
    )
    ids2_far = from_behind(ids2, "dom", -2)
    ids2 = jnp.where(odd, ids2_far, ids2)

    live2 = (slot_ids < ids2[4]).astype(jnp.float32)
    lhs_block2 = jnp.where(odd, other_block2, own_block)
    rhs_block2 = jnp.where(odd, own_block, other_block2)
    lhs_grad2, rhs_grad2 = block_grads(
        lhs_block2,
        rhs_block2,
        relation_diag,
        local_rows(ids2[0]),
        local_rows(ids2[1]),
        ids2[2],
        local_rows(ids2[3]),
        live2,
    )
    keep2 = jnp.where(odd, rhs_grad2, lhs_grad2)
    send2 = jnp.where(odd, lhs_grad2, rhs_grad2)
    recv2 = parity_return(send2.astype(jnp.bfloat16), "dom", 2).astype(jnp.float32)

    live1 = (slot_ids < bucket_counts[0, 0]).astype(jnp.float32)
    lhs_grad1, rhs_grad1 = block_grads(
        own_block,
        rhs_block1,
        relation_diag,
        local_rows(src_index[0, 0]),
        local_rows(dst_index[0, 0]),
        rel_index[0, 0],
        local_rows(neg_index[0, 0, 0]),
        live1,
    )
    recv1 = from_behind(rhs_grad1.astype(jnp.bfloat16), "dom", -1).astype(jnp.float32)

    stacked_total = lhs_grad1 + keep2 + recv1 + recv2
    grad_total = group_reduce_scatter(stacked_total, quarter)
    new_state = adagrad_state + jnp.mean(grad_total * grad_total, axis=1)
    new_embeddings = embeddings - LEARN_RATE * grad_total / (jnp.sqrt(new_state)[:, None] + ROW_EPS)
    return (new_embeddings, new_state)


def solution(mesh):
    placed = (
        P(("dom", "group"), None),
        P(("dom", "group")),
        P(),
        P(None, "dom"),
        P(None, "dom", "group"),
        P(None, "dom", "group"),
        P(None, "dom", "group"),
        P(None, "dom", "group", None),
    )
    return jax.shard_map(
        per_device,
        mesh=mesh,
        in_specs=placed,
        out_specs=(P(("dom", "group"), None), P(("dom", "group"))),
        check_vma=False,
    )
```

```python
import jax
import jax.numpy as jnp
from jax import lax
from jax.sharding import PartitionSpec as P

ROUNDS = 2


LEARN_RATE = 0.1
ROW_EPS = 1e-06


def from_behind(block, axis, distance):
    devices = range(lax.axis_size(axis))
    route = [((i - distance) % len(devices), i) for i in devices]
    return lax.ppermute(block, axis, route)


def parity_swap(block, axis, distance):
    n = lax.axis_size(axis)
    route = [((i - distance) % n, i) if i % 2 == 0 else ((i + distance) % n, i) for i in range(n)]
    return lax.ppermute(block, axis, route)


def parity_return(block, axis, distance):
    n = lax.axis_size(axis)
    route = [(i, (i - distance) % n) if i % 2 == 0 else (i, (i + distance) % n) for i in range(n)]
    return lax.ppermute(block, axis, route)


def group_gather(x):
    half = x.shape[1] // 2
    p1 = from_behind(x, "group", 1)
    p3 = from_behind(x, "group", -1)
    p2a = from_behind(p1[:, :half], "group", 1)
    p2b = from_behind(p3[:, half:], "group", -1)
    return jnp.concatenate([x, p1, p2a, p2b, p3], axis=1)


def group_reduce_scatter(y, quarter):
    half = quarter // 2
    c0, c1, c2, c3 = (y[s * quarter:(s + 1) * quarter] for s in range(4))
    plus_src, minus_src = lax.optimization_barrier(
        (jnp.concatenate([c2[:half], c3[half:]]), jnp.concatenate([c2[half:], c1[:half]]))
    )
    plus1 = from_behind(plus_src.astype(jnp.bfloat16), "group", 1).astype(jnp.float32)
    minus1 = from_behind(minus_src.astype(jnp.bfloat16), "group", -1).astype(jnp.float32)
    plus_next, minus_next, top, bottom = lax.optimization_barrier(
        (plus1[:half] + c3[:half], minus1[:half] + c1[half:],
         c0[:half] + minus1[half:], c0[half:] + plus1[half:])
    )
    plus2 = from_behind(plus_next.astype(jnp.bfloat16), "group", 1).astype(jnp.float32)
    minus2 = from_behind(minus_next.astype(jnp.bfloat16), "group", -1).astype(jnp.float32)
    top = top + plus2
    bottom = bottom + minus2
    return jnp.concatenate([top, bottom], axis=0)


def select_table(row_ids, count):
    return row_ids[:, None] == lax.iota(jnp.int32, count)[None, :]


def pick_rows(table, block):
    return jnp.dot(table.astype(jnp.bfloat16), block, preferred_element_type=jnp.float32).astype(
        jnp.bfloat16
    )


def add_rows(table, values):
    hi_wide = lax.reduce_precision(values, exponent_bits=8, mantissa_bits=7)
    hi = hi_wide.astype(jnp.bfloat16)
    lo = (values - hi_wide).astype(jnp.bfloat16)
    table = table.astype(jnp.bfloat16)
    dims = (((0,), (0,)), ((), ()))
    return lax.dot_general(table, hi, dims, preferred_element_type=jnp.float32) + lax.dot_general(
        table, lo, dims, preferred_element_type=jnp.float32
    )


def block_grads(lhs_block, rhs_block, relation_diag, src_ids, dst_ids, rel_ids, neg_ids, live_mask):
    part_rows = lhs_block.shape[0]
    src_table = select_table(src_ids, part_rows)
    edges = dst_ids.shape[0]
    right_table = select_table(jnp.concatenate([dst_ids, neg_ids]), part_rows)
    dst_table = right_table[:edges]
    neg_table = right_table[edges:]
    lhs_rows = pick_rows(src_table, lhs_block)
    right_rows = pick_rows(right_table, rhs_block)
    rhs_rows = right_rows[:edges]
    neg_rows = right_rows[edges:]
    relation_count = relation_diag.shape[0]
    onehot = select_table(rel_ids, relation_count).astype(jnp.float32)
    rel_rows = jnp.dot(onehot, relation_diag, precision=lax.Precision.HIGHEST)
    query_rows = lhs_rows.astype(jnp.float32) * rel_rows
    query_half = query_rows.astype(jnp.bfloat16)
    rhs_wide = rhs_rows.astype(jnp.float32)
    pos_score = jnp.sum(query_rows * rhs_wide, axis=1)
    scores = lax.dot_general(
        query_half, neg_rows, (((1,), (1,)), ((), ())), preferred_element_type=jnp.float32
    )
    weights = (live_mask[:, None] * jax.nn.sigmoid(scores) / neg_ids.shape[0]).astype(jnp.bfloat16)
    pos_coef = -live_mask * jax.nn.sigmoid(-pos_score)
    grad_query = pos_coef[:, None] * rhs_wide + jnp.dot(
        weights, neg_rows, preferred_element_type=jnp.float32
    )
    grad_neg = lax.dot_general(
        weights, query_half, (((0,), (0,)), ((), ())), preferred_element_type=jnp.float32
    )
    lhs_grad = add_rows(src_table, grad_query * rel_rows)
    rhs_grad = add_rows(dst_table, pos_coef[:, None] * query_rows) + add_rows(neg_table, grad_neg)
    return (lhs_grad, rhs_grad)


def per_device(
    embeddings,
    adagrad_state,
    relation_diag,
    bucket_counts,
    src_index,
    dst_index,
    rel_index,
    neg_index,
):
    emb_half = embeddings.astype(jnp.bfloat16)
    quarter = emb_half.shape[0]
    n_group = lax.axis_size("group")
    part_rows = n_group * quarter
    g = lax.axis_index("group")
    odd = (lax.axis_index("dom") % 2) == 1

    def local_rows(ids):
        return ((g - ids // quarter) % n_group) * quarter + ids % quarter

    edge_slots = src_index.shape[2]
    slot_ids = g * edge_slots + lax.iota(jnp.int32, edge_slots)

    own_block = group_gather(emb_half[None])[0]
    other2 = parity_swap(emb_half, "dom", 2)
    other_block2 = group_gather(other2[None])[0]
    rhs_block1 = from_behind(own_block, "dom", 1)

    ids2 = jnp.stack(
        [src_index[1, 0], dst_index[1, 0], rel_index[1, 0], neg_index[1, 0, 0],
         jnp.broadcast_to(bucket_counts[1, 0], (edge_slots,))]
    )
    ids2_far = from_behind(ids2, "dom", -2)
    ids2 = jnp.where(odd, ids2_far, ids2)

    live2 = (slot_ids < ids2[4]).astype(jnp.float32)
    lhs_block2 = jnp.where(odd, other_block2, own_block)
    rhs_block2 = jnp.where(odd, own_block, other_block2)
    lhs_grad2, rhs_grad2 = block_grads(
        lhs_block2,
        rhs_block2,
        relation_diag,
        local_rows(ids2[0]),
        local_rows(ids2[1]),
        ids2[2],
        local_rows(ids2[3]),
        live2,
    )
    keep2 = jnp.where(odd, rhs_grad2, lhs_grad2)
    send2 = jnp.where(odd, lhs_grad2, rhs_grad2)
    recv2 = parity_return(send2.astype(jnp.bfloat16), "dom", 2).astype(jnp.float32)

    live1 = (slot_ids < bucket_counts[0, 0]).astype(jnp.float32)
    lhs_grad1, rhs_grad1 = block_grads(
        own_block,
        rhs_block1,
        relation_diag,
        local_rows(src_index[0, 0]),
        local_rows(dst_index[0, 0]),
        rel_index[0, 0],
        local_rows(neg_index[0, 0, 0]),
        live1,
    )
    recv1 = from_behind(rhs_grad1.astype(jnp.bfloat16), "dom", -1).astype(jnp.float32)

    stacked_total = lhs_grad1 + keep2 + recv1 + recv2
    grad_total = group_reduce_scatter(stacked_total, quarter)
    new_state = adagrad_state + jnp.mean(grad_total * grad_total, axis=1)
    new_embeddings = embeddings - LEARN_RATE * grad_total / (jnp.sqrt(new_state)[:, None] + ROW_EPS)
    return (new_embeddings, new_state)


def solution(mesh):
    placed = (
        P(("dom", "group"), None),
        P(("dom", "group")),
        P(),
        P(None, "dom"),
        P(None, "dom", "group"),
        P(None, "dom", "group"),
        P(None, "dom", "group"),
        P(None, "dom", "group", None),
    )
    return jax.shard_map(
        per_device,
        mesh=mesh,
        in_specs=placed,
        out_specs=(P(("dom", "group"), None), P(("dom", "group"))),
        check_vma=False,
    )
```

```python
import jax
import jax.numpy as jnp
from jax import lax
from jax.sharding import PartitionSpec as P

ROUNDS = 2


LEARN_RATE = 0.1
ROW_EPS = 1e-06


def from_behind(block, axis, distance):
    devices = range(lax.axis_size(axis))
    route = [((i - distance) % len(devices), i) for i in devices]
    return lax.ppermute(block, axis, route)


def parity_swap(block, axis, distance):
    n = lax.axis_size(axis)
    route = [((i - distance) % n, i) if i % 2 == 0 else ((i + distance) % n, i) for i in range(n)]
    return lax.ppermute(block, axis, route)


def parity_return(block, axis, distance):
    n = lax.axis_size(axis)
    route = [(i, (i - distance) % n) if i % 2 == 0 else (i, (i + distance) % n) for i in range(n)]
    return lax.ppermute(block, axis, route)


def group_gather(x):
    half = x.shape[1] // 2
    p1 = from_behind(x, "group", 1)
    p3 = from_behind(x, "group", -1)
    p2a = from_behind(p1[:, :half], "group", 1)
    p2b = from_behind(p3[:, half:], "group", -1)
    return jnp.concatenate([x, p1, p2a, p2b, p3], axis=1)


def group_reduce_scatter(y, quarter):
    half = quarter // 2
    c0, c1, c2, c3 = (y[s * quarter:(s + 1) * quarter] for s in range(4))
    plus_src, minus_src = lax.optimization_barrier(
        (jnp.concatenate([c2[:half], c3[half:]]), jnp.concatenate([c2[half:], c1[:half]]))
    )
    plus1 = from_behind(plus_src.astype(jnp.bfloat16), "group", 1).astype(jnp.float32)
    minus1 = from_behind(minus_src.astype(jnp.bfloat16), "group", -1).astype(jnp.float32)
    plus_next, minus_next, top, bottom = lax.optimization_barrier(
        (plus1[:half] + c3[:half], minus1[:half] + c1[half:],
         c0[:half] + minus1[half:], c0[half:] + plus1[half:])
    )
    plus2 = from_behind(plus_next.astype(jnp.bfloat16), "group", 1).astype(jnp.float32)
    minus2 = from_behind(minus_next.astype(jnp.bfloat16), "group", -1).astype(jnp.float32)
    top = top + plus2
    bottom = bottom + minus2
    return jnp.concatenate([top, bottom], axis=0)


def select_table(row_ids, count):
    return row_ids[:, None] == lax.iota(jnp.int32, count)[None, :]


def pick_rows(table, block):
    return jnp.dot(table.astype(jnp.bfloat16), block, preferred_element_type=jnp.float32).astype(
        jnp.bfloat16
    )


def add_rows(table, values):
    hi_wide = lax.reduce_precision(values, exponent_bits=8, mantissa_bits=7)
    hi = hi_wide.astype(jnp.bfloat16)
    lo = (values - hi_wide).astype(jnp.bfloat16)
    table = table.astype(jnp.bfloat16)
    dims = (((0,), (0,)), ((), ()))
    return lax.dot_general(table, hi, dims, preferred_element_type=jnp.float32) + lax.dot_general(
        table, lo, dims, preferred_element_type=jnp.float32
    )


def block_grads(lhs_block, rhs_block, relation_diag, src_ids, dst_ids, rel_ids, neg_ids, live_mask):
    part_rows = lhs_block.shape[0]
    src_table = select_table(src_ids, part_rows)
    dst_table = select_table(dst_ids, part_rows)
    neg_table = select_table(neg_ids, part_rows)
    lhs_rows = pick_rows(src_table, lhs_block)
    rhs_rows = pick_rows(dst_table, rhs_block)
    neg_rows = pick_rows(neg_table, rhs_block)
    relation_count = relation_diag.shape[0]
    onehot = select_table(rel_ids, relation_count).astype(jnp.float32)
    rel_rows = jnp.dot(onehot, relation_diag, precision=lax.Precision.HIGHEST)
    query_rows = lhs_rows.astype(jnp.float32) * rel_rows
    query_half = query_rows.astype(jnp.bfloat16)
    rhs_wide = rhs_rows.astype(jnp.float32)
    pos_score = jnp.sum(query_rows * rhs_wide, axis=1)
    scores = lax.dot_general(
        query_half, neg_rows, (((1,), (1,)), ((), ())), preferred_element_type=jnp.float32
    )
    weights = (live_mask[:, None] * jax.nn.sigmoid(scores) / neg_ids.shape[0]).astype(jnp.bfloat16)
    pos_coef = -live_mask * jax.nn.sigmoid(-pos_score)
    grad_query = pos_coef[:, None] * rhs_wide + jnp.dot(
        weights, neg_rows, preferred_element_type=jnp.float32
    )
    grad_neg = lax.dot_general(
        weights, query_half, (((0,), (0,)), ((), ())), preferred_element_type=jnp.float32
    )
    lhs_grad = add_rows(src_table, grad_query * rel_rows)
    rhs_grad = add_rows(dst_table, pos_coef[:, None] * query_rows) + add_rows(neg_table, grad_neg)
    return (lhs_grad, rhs_grad)


def per_device(
    embeddings,
    adagrad_state,
    relation_diag,
    bucket_counts,
    src_index,
    dst_index,
    rel_index,
    neg_index,
):
    emb_half = lax.optimization_barrier(embeddings.astype(jnp.bfloat16))
    quarter = emb_half.shape[0]
    n_group = lax.axis_size("group")
    part_rows = n_group * quarter
    g = lax.axis_index("group")
    odd = (lax.axis_index("dom") % 2) == 1

    def local_rows(ids):
        return ((g - ids // quarter) % n_group) * quarter + ids % quarter

    edge_slots = src_index.shape[2]
    slot_ids = g * edge_slots + lax.iota(jnp.int32, edge_slots)

    own_block = group_gather(emb_half[None])[0]
    other2 = parity_swap(emb_half, "dom", 2)
    other_block2 = group_gather(other2[None])[0]
    rhs_block1 = from_behind(own_block, "dom", 1)

    ids2 = jnp.stack(
        [src_index[1, 0], dst_index[1, 0], rel_index[1, 0], neg_index[1, 0, 0],
         jnp.broadcast_to(bucket_counts[1, 0], (edge_slots,))]
    )
    ids2_far = from_behind(ids2, "dom", -2)
    ids2 = jnp.where(odd, ids2_far, ids2)

    live2 = (slot_ids < ids2[4]).astype(jnp.float32)
    lhs_block2 = jnp.where(odd, other_block2, own_block)
    rhs_block2 = jnp.where(odd, own_block, other_block2)
    lhs_grad2, rhs_grad2 = block_grads(
        lhs_block2,
        rhs_block2,
        relation_diag,
        local_rows(ids2[0]),
        local_rows(ids2[1]),
        ids2[2],
        local_rows(ids2[3]),
        live2,
    )
    keep2 = jnp.where(odd, rhs_grad2, lhs_grad2)
    send2 = jnp.where(odd, lhs_grad2, rhs_grad2)
    recv2 = parity_return(send2.astype(jnp.bfloat16), "dom", 2).astype(jnp.float32)

    live1 = (slot_ids < bucket_counts[0, 0]).astype(jnp.float32)
    lhs_grad1, rhs_grad1 = block_grads(
        own_block,
        rhs_block1,
        relation_diag,
        local_rows(src_index[0, 0]),
        local_rows(dst_index[0, 0]),
        rel_index[0, 0],
        local_rows(neg_index[0, 0, 0]),
        live1,
    )
    recv1 = from_behind(rhs_grad1.astype(jnp.bfloat16), "dom", -1).astype(jnp.float32)

    stacked_total = lhs_grad1 + keep2 + recv1 + recv2
    grad_total = group_reduce_scatter(stacked_total, quarter)
    new_state = adagrad_state + jnp.mean(grad_total * grad_total, axis=1)
    new_embeddings = embeddings - LEARN_RATE * grad_total / (jnp.sqrt(new_state)[:, None] + ROW_EPS)
    return (new_embeddings, new_state)


def solution(mesh):
    placed = (
        P(("dom", "group"), None),
        P(("dom", "group")),
        P(),
        P(None, "dom"),
        P(None, "dom", "group"),
        P(None, "dom", "group"),
        P(None, "dom", "group"),
        P(None, "dom", "group", None),
    )
    return jax.shard_map(
        per_device,
        mesh=mesh,
        in_specs=placed,
        out_specs=(P(("dom", "group"), None), P(("dom", "group"))),
        check_vma=False,
    )
```

```python
import jax
import jax.numpy as jnp
from jax import lax
from jax.sharding import PartitionSpec as P

ROUNDS = 2


LEARN_RATE = 0.1
ROW_EPS = 1e-06


def from_behind(block, axis, distance):
    devices = range(lax.axis_size(axis))
    route = [((i - distance) % len(devices), i) for i in devices]
    return lax.ppermute(block, axis, route)


def parity_swap(block, axis, distance):
    n = lax.axis_size(axis)
    route = [((i - distance) % n, i) if i % 2 == 0 else ((i + distance) % n, i) for i in range(n)]
    return lax.ppermute(block, axis, route)


def parity_return(block, axis, distance):
    n = lax.axis_size(axis)
    route = [(i, (i - distance) % n) if i % 2 == 0 else (i, (i + distance) % n) for i in range(n)]
    return lax.ppermute(block, axis, route)


def group_gather(x):
    half = x.shape[1] // 2
    p1 = from_behind(x, "group", 1)
    p3 = from_behind(x, "group", -1)
    p2a = from_behind(p1[:, :half], "group", 1)
    p2b = from_behind(p3[:, half:], "group", -1)
    return jnp.concatenate([x, p1, p2a, p2b, p3], axis=1)


def group_reduce_scatter(y, quarter):
    half = quarter // 2
    c0, c1, c2, c3 = (y[s * quarter:(s + 1) * quarter] for s in range(4))
    plus_src, minus_src = lax.optimization_barrier(
        (jnp.concatenate([c2[:half], c3[half:]]), jnp.concatenate([c2[half:], c1[:half]]))
    )
    plus1 = from_behind(plus_src.astype(jnp.bfloat16), "group", 1).astype(jnp.float32)
    minus1 = from_behind(minus_src.astype(jnp.bfloat16), "group", -1).astype(jnp.float32)
    plus_next, minus_next, top, bottom = lax.optimization_barrier(
        (plus1[:half] + c3[:half], minus1[:half] + c1[half:],
         c0[:half] + minus1[half:], c0[half:] + plus1[half:])
    )
    plus2 = from_behind(plus_next.astype(jnp.bfloat16), "group", 1).astype(jnp.float32)
    minus2 = from_behind(minus_next.astype(jnp.bfloat16), "group", -1).astype(jnp.float32)
    top = top + plus2
    bottom = bottom + minus2
    return jnp.concatenate([top, bottom], axis=0)


def select_table(row_ids, count):
    return row_ids[:, None] == lax.iota(jnp.int32, count)[None, :]


def pick_rows(table, block):
    return jnp.dot(table.astype(jnp.bfloat16), block, preferred_element_type=jnp.float32).astype(
        jnp.bfloat16
    )


def add_rows(table, values):
    hi_wide = lax.reduce_precision(values, exponent_bits=8, mantissa_bits=7)
    hi = hi_wide.astype(jnp.bfloat16)
    lo = (values - hi_wide).astype(jnp.bfloat16)
    table = table.astype(jnp.bfloat16)
    dims = (((0,), (0,)), ((), ()))
    return lax.dot_general(table, hi, dims, preferred_element_type=jnp.float32) + lax.dot_general(
        table, lo, dims, preferred_element_type=jnp.float32
    )


def block_grads(lhs_block, rhs_block, relation_diag, src_ids, dst_ids, rel_ids, neg_ids, live_mask):
    part_rows = lhs_block.shape[0]
    src_table = select_table(src_ids, part_rows)
    dst_table = select_table(dst_ids, part_rows)
    neg_table = select_table(neg_ids, part_rows)
    lhs_rows = pick_rows(src_table, lhs_block)
    rhs_rows = pick_rows(dst_table, rhs_block)
    neg_rows = pick_rows(neg_table, rhs_block)
    relation_count = relation_diag.shape[0]
    onehot = select_table(rel_ids, relation_count).astype(jnp.float32)
    rel_rows = jnp.dot(onehot, relation_diag, precision=lax.Precision.HIGHEST)
    query_rows = lhs_rows.astype(jnp.float32) * rel_rows
    query_half = query_rows.astype(jnp.bfloat16)
    rhs_wide = rhs_rows.astype(jnp.float32)
    pos_score = jnp.sum(query_rows * rhs_wide, axis=1)
    scores = lax.dot_general(
        query_half, neg_rows, (((1,), (1,)), ((), ())), preferred_element_type=jnp.float32
    )
    weights = (live_mask[:, None] * jax.nn.sigmoid(scores) / neg_ids.shape[0]).astype(jnp.bfloat16)
    pos_coef = -live_mask * jax.nn.sigmoid(-pos_score)
    grad_query = pos_coef[:, None] * rhs_wide + jnp.dot(
        weights, neg_rows, preferred_element_type=jnp.float32
    )
    grad_neg = lax.dot_general(
        weights, query_half, (((0,), (0,)), ((), ())), preferred_element_type=jnp.float32
    )
    lhs_grad = add_rows(src_table, grad_query * rel_rows)
    rhs_grad = add_rows(dst_table, pos_coef[:, None] * query_rows) + add_rows(neg_table, grad_neg)
    return (lhs_grad, rhs_grad)


def per_device(
    embeddings,
    adagrad_state,
    relation_diag,
    bucket_counts,
    src_index,
    dst_index,
    rel_index,
    neg_index,
):
    emb_half = lax.optimization_barrier(embeddings.astype(jnp.bfloat16))
    quarter = emb_half.shape[0]
    n_group = lax.axis_size("group")
    part_rows = n_group * quarter
    g = lax.axis_index("group")
    odd = (lax.axis_index("dom") % 2) == 1

    def local_rows(ids):
        return ((g - ids // quarter) % n_group) * quarter + ids % quarter

    edge_slots = src_index.shape[2]
    slot_ids = g * edge_slots + lax.iota(jnp.int32, edge_slots)

    own_block = group_gather(emb_half[None])[0]
    other2 = parity_swap(emb_half, "dom", 2)
    other_block2 = group_gather(other2[None])[0]
    rhs_block1 = from_behind(own_block, "dom", 1)

    ids2 = jnp.stack(
        [src_index[1, 0], dst_index[1, 0], rel_index[1, 0], neg_index[1, 0, 0],
         jnp.broadcast_to(bucket_counts[1, 0], (edge_slots,))]
    )
    ids2_far = from_behind(ids2, "dom", -2)
    ids2 = jnp.where(odd, ids2_far, ids2)

    live2 = (slot_ids < ids2[4]).astype(jnp.float32)
    lhs_block2 = jnp.where(odd, other_block2, own_block)
    rhs_block2 = jnp.where(odd, own_block, other_block2)
    lhs_grad2, rhs_grad2 = block_grads(
        lhs_block2,
        rhs_block2,
        relation_diag,
        local_rows(ids2[0]),
        local_rows(ids2[1]),
        ids2[2],
        local_rows(ids2[3]),
        live2,
    )
    keep2 = jnp.where(odd, rhs_grad2, lhs_grad2)
    send2 = jnp.where(odd, lhs_grad2, rhs_grad2)
    recv2 = parity_return(send2.astype(jnp.bfloat16), "dom", 2).astype(jnp.float32)

    live1 = (slot_ids < bucket_counts[0, 0]).astype(jnp.float32)
    lhs_grad1, rhs_grad1 = block_grads(
        own_block,
        rhs_block1,
        relation_diag,
        local_rows(src_index[0, 0]),
        local_rows(dst_index[0, 0]),
        rel_index[0, 0],
        local_rows(neg_index[0, 0, 0]),
        live1,
    )
    recv1 = from_behind(rhs_grad1.astype(jnp.bfloat16), "dom", -1).astype(jnp.float32)

    early_total = lax.optimization_barrier(lhs_grad1 + keep2 + recv2)
    stacked_total = early_total + recv1
    grad_total = group_reduce_scatter(stacked_total, quarter)
    new_state = adagrad_state + jnp.mean(grad_total * grad_total, axis=1)
    new_embeddings = embeddings - LEARN_RATE * grad_total / (jnp.sqrt(new_state)[:, None] + ROW_EPS)
    return (new_embeddings, new_state)


def solution(mesh):
    placed = (
        P(("dom", "group"), None),
        P(("dom", "group")),
        P(),
        P(None, "dom"),
        P(None, "dom", "group"),
        P(None, "dom", "group"),
        P(None, "dom", "group"),
        P(None, "dom", "group", None),
    )
    return jax.shard_map(
        per_device,
        mesh=mesh,
        in_specs=placed,
        out_specs=(P(("dom", "group"), None), P(("dom", "group"))),
        check_vma=False,
    )
```
